512 devices in a mesh: src: 16 (over y_hi, x, core), rcv: 32 (over y_lo, z).
Axes of the slice: x: 4, y: 8 (y_hi: 2, y_lo: 4; y = y_hi * 4 + y_lo), z: 8, core: 2. Of those that a mesh axis runs over, the one named last changes fastest.
Arguments:
- observed: bfloat16 [1024, 1024, 64], P('src', 'rcv'), may hold values from -6 to 6
- estimate: bfloat16 [1024, 1024, 64], P('src', 'rcv'), may hold values from -6 to 6
- acquired: int32 [8, 8], replicated, may hold values 0 or 1
- levels: int32 [2, 64], replicated, may hold values from 1 to 3, as said below
- thresholds: float32 [64], replicated, may hold values from 0.05 to 0.6
Outputs:
- refined: float32 [1024, 1024, 64], P('src', 'rcv')
The draws below stay inside these ranges and needn't reach their ends.
Inputs may be any that keep to these rules, and one draw needn't show every extreme that they name: `levels`: in each time sample one of the two entries equals 3 and the other is smaller.
All inputs are finite; a program needn't handle non-finite values.
Results may differ from the reference program's by a relative error of at most 0.0015.
Values may be sent and summed in bfloat16 or wider, within the bound.
No kernel may reach another device: no remote copies, remote signals or barrier semaphores. Data moves between devices by JAX's collectives and lax.ppermute only.
A program may use at most 64 MiB of HBM per device.

```python
import math
import jax
import jax.numpy as jnp
from jax import lax

T_SIZE = 64
BLK = 128
LEVELS = 3
S = 1024
NB = 8


def draw_levels(key, part):
    key_pick = jax.random.fold_in(key, 11)
    key_second = jax.random.fold_in(key, 12)
    chosen = jax.random.randint(key_pick, (1, T_SIZE), 0, 2)
    second = jax.random.randint(key_second, (1, T_SIZE), 1, LEVELS)
    entry_ids = jnp.arange(2, dtype=jnp.int32)[:, None]
    return jnp.where(entry_ids == chosen, LEVELS, second).astype(jnp.int32)


def with_ends(entries, key, smallest, largest):
    longest = entries.shape.index(max(entries.shape))
    spots = []
    for shift in (0, 1):
        where = [jax.random.randint(jax.random.fold_in(key, axis), (), 0, length) for axis, length in enumerate(entries.shape)]
        where[longest] = (where[longest] + shift) % entries.shape[longest]
        spots.append(tuple(where))
    return entries.at[spots[0]].set(smallest).at[spots[1]].set(largest)


def block_levels(stream_key, shape, pieces, least, largest):
    gain = 1.0
    for dim, parts in pieces:
        heights = jax.random.uniform(jax.random.fold_in(jax.random.fold_in(stream_key, 6), dim), (parts,), jnp.float32, least / len(pieces), largest / len(pieces))
        gain = gain * jnp.repeat(jnp.exp(heights), shape[dim] // parts).reshape((-1,) + (1,) * (len(shape) - 1 - dim))
    return gain


def scatter_about(key, shape, width, bound, split=(), held_as=jnp.bfloat16):
    array = width * jax.random.normal(key, shape, jnp.float32)
    if split:
        array = array * block_levels(key, shape, split, -0.22, 0.18)
    return jnp.clip(array, -bound, bound).astype(held_as)


def setup_inputs(seed: int = 0) -> dict:
    splits = jax.random.split(jax.random.key(seed), 6)
    observed = scatter_about(splits[0], (S, S, T_SIZE), 1.0, 6.0, ((0, 16), (1, 32)))
    estimate = scatter_about(splits[1], (S, S, T_SIZE), 1.0, 6.0, ((0, 16), (1, 32)))
    acquired = with_ends((jax.random.randint(splits[2], (NB, NB), 0, 2) < 1).astype(jnp.int32), jax.random.fold_in(splits[2], 1), 0, 1)
    levels = draw_levels(jax.random.fold_in(splits[5], 71), 0)
    thresholds = jnp.clip(jnp.exp(jax.random.uniform(splits[4], (T_SIZE,), jnp.float32, math.log(0.05), math.log(0.6))), 0.05, 0.6)
    return {"observed": observed, "estimate": estimate, "acquired": acquired, "levels": levels, "thresholds": thresholds}


def split_pairs(field, stride):
    length = field.shape[0]
    shaped = field.reshape((length // (2 * stride), 2, stride) + field.shape[1:])
    return shaped, shaped[:, :, 0]


def join_pairs(shaped, new_pairs, field):
    joined = jnp.concatenate([new_pairs[:, :, None], shaped[:, :, 1:]], axis=2)
    return joined.reshape(field.shape)


def forward_core(pair_rows, left_pair, right_pair, is_first, is_last):
    even_part = pair_rows[:, 0]
    odd_part = pair_rows[:, 1]
    right_even = jnp.where(is_last, even_part[-1], right_pair[0])
    next_even = jnp.concatenate([even_part[1:], right_even[None]], axis=0)
    detail = odd_part - 0.5 * (even_part + next_even)
    left_detail = jnp.where(is_first, detail[0], left_pair[1] - 0.5 * (left_pair[0] + even_part[0]))
    prev_detail = jnp.concatenate([left_detail[None], detail[:-1]], axis=0)
    smooth = even_part + 0.25 * (prev_detail + detail)
    return jnp.stack([smooth, detail], axis=1)


def inverse_core(pair_rows, left_pair, right_pair, is_first, is_last):
    smooth = pair_rows[:, 0]
    detail = pair_rows[:, 1]
    left_detail = jnp.where(is_first, detail[0], left_pair[1])
    prev_detail = jnp.concatenate([left_detail[None], detail[:-1]], axis=0)
    even_part = smooth - 0.25 * (prev_detail + detail)
    right_even = jnp.where(is_last, even_part[-1], right_pair[0] - 0.25 * (detail[-1] + right_pair[1]))
    next_even = jnp.concatenate([even_part[1:], right_even[None]], axis=0)
    odd_part = detail + 0.5 * (even_part + next_even)
    return jnp.stack([even_part, odd_part], axis=1)


def whole_level(field, stride, enabled, forward):
    shaped, pair_rows = split_pairs(field, stride)
    if forward:
        new_pairs = forward_core(pair_rows, pair_rows[0], pair_rows[-1], True, True)
    else:
        new_pairs = inverse_core(pair_rows, pair_rows[0], pair_rows[-1], True, True)
    return jnp.where(enabled, join_pairs(shaped, new_pairs, field), field)


def reference(observed, estimate, acquired, levels, thresholds):
    extent = observed.shape[0]
    samples = observed.shape[2]
    time_block = 8
    count = samples // time_block
    mask_full = jnp.repeat(jnp.repeat(acquired.astype(jnp.float32), BLK, axis=0), BLK, axis=1)

    def one_block(inputs):
        obs_part, est_part, thr_part, lev_part = inputs
        est_float = est_part.astype(jnp.float32)
        merged = (est_float + mask_full[:, :, None] * (obs_part.astype(jnp.float32) - est_float)).astype(jnp.bfloat16)
        merged_float = merged.astype(jnp.float32)
        coeff = 0.5 * (merged_float + jnp.transpose(merged_float, (1, 0, 2)))
        for depth_index in range(LEVELS):
            coeff = whole_level(coeff, 2 ** depth_index, depth_index < lev_part[0], True)
        turned = jnp.moveaxis(coeff, 1, 0)
        for depth_index in range(LEVELS):
            turned = whole_level(turned, 2 ** depth_index, depth_index < lev_part[1], True)
        turned = jnp.sign(turned) * jnp.maximum(jnp.abs(turned) - thr_part, 0.0)
        for depth_index in reversed(range(LEVELS)):
            turned = whole_level(turned, 2 ** depth_index, depth_index < lev_part[1], False)
        coeff = jnp.moveaxis(turned, 0, 1)
        for depth_index in reversed(range(LEVELS)):
            coeff = whole_level(coeff, 2 ** depth_index, depth_index < lev_part[0], False)
        return coeff

    obs_blocks = observed.reshape(extent, extent, count, time_block).transpose(2, 0, 1, 3)
    est_blocks = estimate.reshape(extent, extent, count, time_block).transpose(2, 0, 1, 3)
    thr_blocks = thresholds.reshape(count, time_block)
    lev_blocks = levels.reshape(2, count, time_block).transpose(1, 0, 2)
    result = lax.map(one_block, (obs_blocks, est_blocks, thr_blocks, lev_blocks))
    return result.transpose(1, 2, 0, 3).reshape(extent, extent, samples)
```

```python
import jax
import jax.numpy as jnp
from jax import lax
from jax.sharding import PartitionSpec as P

LEVELS = 3
SRC_HALO = 16
RCV_HALO = 24


def split_pairs(field, stride):
    length = field.shape[0]
    shaped = field.reshape((length // (2 * stride), 2, stride) + field.shape[1:])
    return (shaped, shaped[:, :, 0])


def join_pairs(shaped, new_pairs, field):
    joined = jnp.concatenate([new_pairs[:, :, None], shaped[:, :, 1:]], axis=2)
    return joined.reshape(field.shape)


def forward_core(pair_rows, first, last):
    even_part = pair_rows[:, 0]
    odd_part = pair_rows[:, 1]
    next_even = jnp.concatenate([even_part[1:], even_part[-1:]], axis=0)
    next_even = jnp.where(last, even_part, next_even)
    detail = odd_part - 0.5 * (even_part + next_even)
    prev_detail = jnp.concatenate([detail[:1], detail[:-1]], axis=0)
    prev_detail = jnp.where(first, detail, prev_detail)
    smooth = even_part + 0.25 * (prev_detail + detail)
    return jnp.stack([smooth, detail], axis=1)


def inverse_core(pair_rows, first, last):
    smooth = pair_rows[:, 0]
    detail = pair_rows[:, 1]
    prev_detail = jnp.concatenate([detail[:1], detail[:-1]], axis=0)
    prev_detail = jnp.where(first, detail, prev_detail)
    even_part = smooth - 0.25 * (prev_detail + detail)
    next_even = jnp.concatenate([even_part[1:], even_part[-1:]], axis=0)
    next_even = jnp.where(last, even_part, next_even)
    odd_part = detail + 0.5 * (even_part + next_even)
    return jnp.stack([even_part, odd_part], axis=1)


def level(field, stride, enabled, forward, width, length, is_first, is_last):
    shaped, pair_rows = split_pairs(field, stride)
    pair_ids = jnp.arange(pair_rows.shape[0], dtype=jnp.int32).reshape(
        (-1,) + (1,) * (pair_rows.ndim - 2)
    )
    first = is_first & (pair_ids == width // (2 * stride))
    last = is_last & (pair_ids == (width + length) // (2 * stride) - 1)
    core = forward_core if forward else inverse_core
    new_pairs = core(pair_rows, first, last)
    return jnp.where(enabled, join_pairs(shaped, new_pairs, field), field)


def extend(cells, axis_name, dim, width):
    count = lax.axis_size(axis_name)
    length = cells.shape[dim]
    head = lax.slice_in_dim(cells, 0, width, axis=dim)
    tail = lax.slice_in_dim(cells, length - width, length, axis=dim)
    from_left = lax.ppermute(tail, axis_name, [(i, i + 1) for i in range(count - 1)])
    from_right = lax.ppermute(head, axis_name, [(i + 1, i) for i in range(count - 1)])
    return jnp.concatenate([from_left, cells, from_right], axis=dim)


def body(observed, estimate, acquired, levels, thresholds):
    src_count = lax.axis_size("src")
    rcv_count = lax.axis_size("rcv")
    src_index = lax.axis_index("src")
    rcv_index = lax.axis_index("rcv")
    row_count, col_count, samples = observed.shape
    extent = row_count * src_count
    blocks = acquired.shape[0]
    block_size = extent // blocks
    block_ids = jnp.arange(blocks, dtype=jnp.int32)
    row_ids = src_index * row_count + jnp.arange(row_count, dtype=jnp.int32)
    col_ids = rcv_index * col_count + jnp.arange(col_count, dtype=jnp.int32)
    pick_rows = (row_ids[:, None] // block_size == block_ids[None, :]).astype(jnp.float32)
    pick_cols = (col_ids[:, None] // block_size == block_ids[None, :]).astype(jnp.float32)
    row_mask = jnp.dot(pick_rows, acquired.astype(jnp.float32), precision=lax.Precision.HIGHEST)
    local_mask = jnp.dot(row_mask, pick_cols.T, precision=lax.Precision.HIGHEST)
    est_float = estimate.astype(jnp.float32)
    merged = (
        est_float + local_mask[:, :, None] * (observed.astype(jnp.float32) - est_float)
    ).astype(jnp.bfloat16)

    ratio = rcv_count // src_count
    pieces = merged.reshape(ratio, col_count, col_count, samples)
    own_part = rcv_index % ratio
    received = []
    for shift in range(ratio):
        perm = []
        for a in range(src_count):
            for b in range(rcv_count):
                part = (b % ratio + shift) % ratio
                perm.append((a * rcv_count + b, (b // ratio) * rcv_count + a * ratio + part))
        send = lax.dynamic_index_in_dim(pieces, (own_part + shift) % ratio, axis=0, keepdims=False)
        received.append(lax.ppermute(send, ("src", "rcv"), perm))
    received = jnp.stack(received)
    slots = []
    for slot in range(ratio):
        got = lax.dynamic_index_in_dim(received, (own_part - slot) % ratio, axis=0, keepdims=False)
        slots.append(jnp.transpose(got, (1, 0, 2)))
    mirror = jnp.concatenate(slots, axis=0)
    coeff = 0.5 * (merged.astype(jnp.float32) + mirror.astype(jnp.float32))

    src_levels = levels[0]
    rcv_levels = levels[1]
    src_ends = (src_index == 0, src_index == src_count - 1)
    rcv_ends = (rcv_index == 0, rcv_index == rcv_count - 1)

    wide = extend(coeff, "src", 0, SRC_HALO)
    for depth_index in range(LEVELS):
        wide = level(wide, 2**depth_index, depth_index < src_levels, True, SRC_HALO, row_count, *src_ends)
    coeff = wide[SRC_HALO : SRC_HALO + row_count]

    wide = extend(coeff, "rcv", 1, RCV_HALO)
    turned = jnp.moveaxis(wide, 1, 0)
    for depth_index in range(LEVELS):
        turned = level(turned, 2**depth_index, depth_index < rcv_levels, True, RCV_HALO, col_count, *rcv_ends)
    turned = jnp.sign(turned) * jnp.maximum(jnp.abs(turned) - thresholds, 0.0)
    for depth_index in reversed(range(LEVELS)):
        turned = level(turned, 2**depth_index, depth_index < rcv_levels, False, RCV_HALO, col_count, *rcv_ends)
    coeff = jnp.moveaxis(turned[RCV_HALO : RCV_HALO + col_count], 0, 1)

    wide = extend(coeff, "src", 0, SRC_HALO)
    for depth_index in reversed(range(LEVELS)):
        wide = level(wide, 2**depth_index, depth_index < src_levels, False, SRC_HALO, row_count, *src_ends)
    return wide[SRC_HALO : SRC_HALO + row_count]


def solution(mesh):
    return jax.shard_map(
        body,
        mesh=mesh,
        in_specs=(P("src", "rcv", None), P("src", "rcv", None), P(), P(), P()),
        out_specs=P("src", "rcv", None),
        check_vma=False,
    )
```

```python
import jax
import jax.numpy as jnp
from jax import lax
from jax.sharding import PartitionSpec as P

LEVELS = 3
SRC_HALO = 16
RCV_HALO = 24


def split_pairs(field, stride):
    length = field.shape[0]
    shaped = field.reshape((length // (2 * stride), 2, stride) + field.shape[1:])
    return (shaped, shaped[:, :, 0])


def join_pairs(shaped, new_pairs, field):
    joined = jnp.concatenate([new_pairs[:, :, None], shaped[:, :, 1:]], axis=2)
    return joined.reshape(field.shape)


def forward_core(pair_rows, first, last):
    even_part = pair_rows[:, 0]
    odd_part = pair_rows[:, 1]
    next_even = jnp.concatenate([even_part[1:], even_part[-1:]], axis=0)
    next_even = jnp.where(last, even_part, next_even)
    detail = odd_part - 0.5 * (even_part + next_even)
    prev_detail = jnp.concatenate([detail[:1], detail[:-1]], axis=0)
    prev_detail = jnp.where(first, detail, prev_detail)
    smooth = even_part + 0.25 * (prev_detail + detail)
    return jnp.stack([smooth, detail], axis=1)


def inverse_core(pair_rows, first, last):
    smooth = pair_rows[:, 0]
    detail = pair_rows[:, 1]
    prev_detail = jnp.concatenate([detail[:1], detail[:-1]], axis=0)
    prev_detail = jnp.where(first, detail, prev_detail)
    even_part = smooth - 0.25 * (prev_detail + detail)
    next_even = jnp.concatenate([even_part[1:], even_part[-1:]], axis=0)
    next_even = jnp.where(last, even_part, next_even)
    odd_part = detail + 0.5 * (even_part + next_even)
    return jnp.stack([even_part, odd_part], axis=1)


def level(field, stride, enabled, forward, width, length, is_first, is_last):
    shaped, pair_rows = split_pairs(field, stride)
    pair_ids = jnp.arange(pair_rows.shape[0], dtype=jnp.int32).reshape(
        (-1,) + (1,) * (pair_rows.ndim - 2)
    )
    first = is_first & (pair_ids == width // (2 * stride))
    last = is_last & (pair_ids == (width + length) // (2 * stride) - 1)
    core = forward_core if forward else inverse_core
    new_pairs = core(pair_rows, first, last)
    return jnp.where(enabled, join_pairs(shaped, new_pairs, field), field)


def extend(cells, axis_name, dim, width):
    count = lax.axis_size(axis_name)
    length = cells.shape[dim]
    head = lax.slice_in_dim(cells, 0, width, axis=dim)
    tail = lax.slice_in_dim(cells, length - width, length, axis=dim)
    from_left = lax.ppermute(tail, axis_name, [(i, i + 1) for i in range(count - 1)])
    from_right = lax.ppermute(head, axis_name, [(i + 1, i) for i in range(count - 1)])
    return jnp.concatenate([from_left, cells, from_right], axis=dim)


def body(observed, estimate, acquired, levels, thresholds):
    src_count = lax.axis_size("src")
    rcv_count = lax.axis_size("rcv")
    src_index = lax.axis_index("src")
    rcv_index = lax.axis_index("rcv")
    row_count, col_count, samples = observed.shape
    extent = row_count * src_count
    blocks = acquired.shape[0]
    block_size = extent // blocks
    block_ids = jnp.arange(blocks, dtype=jnp.int32)
    row_ids = src_index * row_count + jnp.arange(row_count, dtype=jnp.int32)
    col_ids = rcv_index * col_count + jnp.arange(col_count, dtype=jnp.int32)
    pick_rows = (row_ids[:, None] // block_size == block_ids[None, :]).astype(jnp.float32)
    pick_cols = (col_ids[:, None] // block_size == block_ids[None, :]).astype(jnp.float32)
    row_mask = jnp.dot(pick_rows, acquired.astype(jnp.float32), precision=lax.Precision.HIGHEST)
    local_mask = jnp.dot(row_mask, pick_cols.T, precision=lax.Precision.HIGHEST)
    est_float = estimate.astype(jnp.float32)
    merged = (
        est_float + local_mask[:, :, None] * (observed.astype(jnp.float32) - est_float)
    ).astype(jnp.bfloat16)

    ratio = rcv_count // src_count
    pieces = merged.reshape(ratio, col_count, col_count, samples)
    own_part = rcv_index % ratio
    everyone = ("src", "rcv")
    received = []
    for shift in range(ratio):
        perm = []
        for a in range(src_count):
            for b in range(rcv_count):
                part = (b % ratio + shift) % ratio
                perm.append((a * rcv_count + b, (b // ratio) * rcv_count + a * ratio + part))
        send = lax.dynamic_index_in_dim(pieces, (own_part + shift) % ratio, axis=0, keepdims=False)
        received.append(lax.ppermute(send, everyone, perm))
    received = jnp.stack(received)
    slots = []
    for slot in range(ratio):
        got = lax.dynamic_index_in_dim(received, (own_part - slot) % ratio, axis=0, keepdims=False)
        slots.append(jnp.transpose(got, (1, 0, 2)))
    mirror = jnp.concatenate(slots, axis=0)

    edges = []
    odd_sender = rcv_index % 2 == 1
    for shift in range(2):
        perm = []
        for a in range(src_count):
            for b in range(rcv_count):
                if b % 2 == 1 and (b + 1) // ratio < src_count:
                    perm.append((a * rcv_count + b, ((b + 1) // ratio) * rcv_count + a * ratio + shift))
                if b % 2 == 0 and b // ratio - 1 >= 0:
                    perm.append((a * rcv_count + b, (b // ratio - 1) * rcv_count + a * ratio + 1 - shift))
        tail = pieces[shift, :, col_count - SRC_HALO :]
        head = pieces[1 - shift, :, :SRC_HALO]
        send = jnp.where(odd_sender, tail, head)
        edges.append(jnp.transpose(lax.ppermute(send, everyone, perm), (1, 0, 2)))
    left_edge = jnp.where(own_part == 0, edges[0], edges[1])
    right_edge = jnp.where(own_part == 0, edges[1], edges[0])
    mirror = jnp.concatenate([left_edge, mirror, right_edge], axis=0)
    merged_wide = extend(merged, "src", 0, SRC_HALO)
    wide = 0.5 * (merged_wide.astype(jnp.float32) + mirror.astype(jnp.float32))

    src_levels = levels[0]
    rcv_levels = levels[1]
    src_ends = (src_index == 0, src_index == src_count - 1)
    rcv_ends = (rcv_index == 0, rcv_index == rcv_count - 1)

    for depth_index in range(LEVELS):
        wide = level(wide, 2**depth_index, depth_index < src_levels, True, SRC_HALO, row_count, *src_ends)
    coeff = wide[SRC_HALO : SRC_HALO + row_count]

    wide = extend(coeff, "rcv", 1, RCV_HALO)
    turned = jnp.moveaxis(wide, 1, 0)
    for depth_index in range(LEVELS):
        turned = level(turned, 2**depth_index, depth_index < rcv_levels, True, RCV_HALO, col_count, *rcv_ends)
    turned = jnp.sign(turned) * jnp.maximum(jnp.abs(turned) - thresholds, 0.0)
    for depth_index in reversed(range(LEVELS)):
        turned = level(turned, 2**depth_index, depth_index < rcv_levels, False, RCV_HALO, col_count, *rcv_ends)
    coeff = jnp.moveaxis(turned[RCV_HALO : RCV_HALO + col_count], 0, 1)

    wide = extend(coeff, "src", 0, SRC_HALO)
    for depth_index in reversed(range(LEVELS)):
        wide = level(wide, 2**depth_index, depth_index < src_levels, False, SRC_HALO, row_count, *src_ends)
    return wide[SRC_HALO : SRC_HALO + row_count]


def solution(mesh):
    return jax.shard_map(
        body,
        mesh=mesh,
        in_specs=(P("src", "rcv", None), P("src", "rcv", None), P(), P(), P()),
        out_specs=P("src", "rcv", None),
        check_vma=False,
    )
```

```python
import functools

import jax
import jax.numpy as jnp
from jax import lax
from jax.sharding import PartitionSpec as P
from jax.experimental import pallas as pl
from jax.experimental.pallas import tpu as pltpu

LEVELS = 3
SRC_HALO = 16
RCV_HALO = 24


def split_pairs(field, stride):
    length = field.shape[0]
    shaped = field.reshape((length // (2 * stride), 2, stride) + field.shape[1:])
    return (shaped, shaped[:, :, 0])


def join_pairs(shaped, new_pairs, field):
    joined = jnp.concatenate([new_pairs[:, :, None], shaped[:, :, 1:]], axis=2)
    return joined.reshape(field.shape)


def forward_core(pair_rows, first, last):
    even_part = pair_rows[:, 0]
    odd_part = pair_rows[:, 1]
    next_even = jnp.concatenate([even_part[1:], even_part[-1:]], axis=0)
    next_even = jnp.where(last, even_part, next_even)
    detail = odd_part - 0.5 * (even_part + next_even)
    prev_detail = jnp.concatenate([detail[:1], detail[:-1]], axis=0)
    prev_detail = jnp.where(first, detail, prev_detail)
    smooth = even_part + 0.25 * (prev_detail + detail)
    return jnp.stack([smooth, detail], axis=1)


def inverse_core(pair_rows, first, last):
    smooth = pair_rows[:, 0]
    detail = pair_rows[:, 1]
    prev_detail = jnp.concatenate([detail[:1], detail[:-1]], axis=0)
    prev_detail = jnp.where(first, detail, prev_detail)
    even_part = smooth - 0.25 * (prev_detail + detail)
    next_even = jnp.concatenate([even_part[1:], even_part[-1:]], axis=0)
    next_even = jnp.where(last, even_part, next_even)
    odd_part = detail + 0.5 * (even_part + next_even)
    return jnp.stack([even_part, odd_part], axis=1)


def level(field, stride, enabled, forward, width, length, is_first, is_last):
    shaped, pair_rows = split_pairs(field, stride)
    pair_ids = jnp.arange(pair_rows.shape[0], dtype=jnp.int32).reshape(
        (-1,) + (1,) * (pair_rows.ndim - 2)
    )
    first = is_first & (pair_ids == width // (2 * stride))
    last = is_last & (pair_ids == (width + length) // (2 * stride) - 1)
    core = forward_core if forward else inverse_core
    new_pairs = core(pair_rows, first, last)
    return jnp.where(enabled, join_pairs(shaped, new_pairs, field), field)


PAD = 8


def _lift_level(work, stride, enabled, forward, width, length, ends):
    rows = work.shape[0] - 2 * PAD
    pairs = rows // (2 * stride)
    step = 2 * stride
    pair_ids = lax.broadcasted_iota(jnp.int32, (pairs,) + work.shape[1:], 0)
    first = (pair_ids == width // step) & (ends[0] != 0)
    last = (pair_ids == (width + length) // step - 1) & (ends[1] != 0)
    evens = pl.ds(PAD, pairs, stride=step)
    odds = pl.ds(PAD + stride, pairs, stride=step)
    next_evens = pl.ds(PAD + step, pairs, stride=step)
    prev_odds = pl.ds(PAD - stride, pairs, stride=step)
    if forward:
        even_part = work[evens]
        odd_part = work[odds]
        next_even = jnp.where(last, even_part, work[next_evens])
        detail = odd_part - 0.5 * (even_part + next_even)
        work[odds] = jnp.where(enabled, detail, odd_part)
        prev_detail = jnp.where(first, detail, work[prev_odds])
        smooth = even_part + 0.25 * (prev_detail + detail)
        work[evens] = jnp.where(enabled, smooth, even_part)
    else:
        smooth = work[evens]
        detail = work[odds]
        prev_detail = jnp.where(first, detail, work[prev_odds])
        even_part = smooth - 0.25 * (prev_detail + detail)
        work[evens] = jnp.where(enabled, even_part, smooth)
        next_even = jnp.where(last, even_part, work[next_evens])
        odd_part = detail + 0.5 * (even_part + next_even)
        work[odds] = jnp.where(enabled, odd_part, detail)


def _stage_kernel(*refs, kind, width, length):
    if kind == "fwd":
        ends_ref, depth_ref, left_ref, right_ref, out_ref, work = refs
    elif kind == "both":
        ends_ref, depth_ref, thr_ref, in_ref, out_ref, work = refs
    else:
        ends_ref, depth_ref, in_ref, out_ref, work = refs
    rows = work.shape[0] - 2 * PAD
    ends = (ends_ref[0], ends_ref[1])
    depth = depth_ref[...]
    if kind == "fwd":
        work[PAD : PAD + rows] = 0.5 * (
            left_ref[...].astype(jnp.float32) + right_ref[...].astype(jnp.float32)
        )
    else:
        work[PAD : PAD + rows] = in_ref[...]
    if kind != "inv":
        for depth_index in range(LEVELS):
            _lift_level(work, 2**depth_index, depth > depth_index, True, width, length, ends)
    if kind == "both":
        field = work[PAD : PAD + rows]
        thr = thr_ref[...]
        work[PAD : PAD + rows] = field - jnp.clip(field, -thr, thr)
    if kind != "fwd":
        for depth_index in reversed(range(LEVELS)):
            _lift_level(work, 2**depth_index, depth > depth_index, False, width, length, ends)
    out_ref[...] = work[PAD + width : PAD + width + length]


def lift_stage(kind, operands, ends, depth, width, length):
    rows, cols, samples = operands[-1].shape
    kernel = functools.partial(_stage_kernel, kind=kind, width=width, length=length)
    smem = pl.BlockSpec(memory_space=pltpu.SMEM)
    vmem = pl.BlockSpec(memory_space=pltpu.VMEM)
    return pl.pallas_call(
        kernel,
        out_shape=jax.ShapeDtypeStruct((length, cols, samples), jnp.float32),
        in_specs=[smem] + [vmem] * (1 + len(operands)),
        out_specs=vmem,
        scratch_shapes=[pltpu.VMEM((rows + 2 * PAD, cols, samples), jnp.float32)],
    )(ends, depth, *operands)


def extend(cells, axis_name, dim, width):
    count = lax.axis_size(axis_name)
    length = cells.shape[dim]
    head = lax.slice_in_dim(cells, 0, width, axis=dim)
    tail = lax.slice_in_dim(cells, length - width, length, axis=dim)
    from_left = lax.ppermute(tail, axis_name, [(i, i + 1) for i in range(count - 1)])
    from_right = lax.ppermute(head, axis_name, [(i + 1, i) for i in range(count - 1)])
    return jnp.concatenate([from_left, cells, from_right], axis=dim)


def body(observed, estimate, acquired, levels, thresholds):
    src_count = lax.axis_size("src")
    rcv_count = lax.axis_size("rcv")
    src_index = lax.axis_index("src")
    rcv_index = lax.axis_index("rcv")
    row_count, col_count, samples = observed.shape
    extent = row_count * src_count
    blocks = acquired.shape[0]
    block_size = extent // blocks
    block_ids = jnp.arange(blocks, dtype=jnp.int32)
    row_ids = src_index * row_count + jnp.arange(row_count, dtype=jnp.int32)
    col_ids = rcv_index * col_count + jnp.arange(col_count, dtype=jnp.int32)
    pick_rows = (row_ids[:, None] // block_size == block_ids[None, :]).astype(jnp.float32)
    pick_cols = (col_ids[:, None] // block_size == block_ids[None, :]).astype(jnp.float32)
    row_mask = jnp.dot(pick_rows, acquired.astype(jnp.float32), precision=lax.Precision.HIGHEST)
    local_mask = jnp.dot(row_mask, pick_cols.T, precision=lax.Precision.HIGHEST)
    est_float = estimate.astype(jnp.float32)
    merged = (
        est_float + local_mask[:, :, None] * (observed.astype(jnp.float32) - est_float)
    ).astype(jnp.bfloat16)

    ratio = rcv_count // src_count
    pieces = merged.reshape(ratio, col_count, col_count, samples)
    own_part = rcv_index % ratio
    received = []
    for shift in range(ratio):
        perm = []
        for a in range(src_count):
            for b in range(rcv_count):
                part = (b % ratio + shift) % ratio
                perm.append((a * rcv_count + b, (b // ratio) * rcv_count + a * ratio + part))
        send = lax.dynamic_index_in_dim(pieces, (own_part + shift) % ratio, axis=0, keepdims=False)
        received.append(lax.ppermute(send, ("src", "rcv"), perm))
    received = jnp.stack(received)
    slots = []
    for slot in range(ratio):
        got = lax.dynamic_index_in_dim(received, (own_part - slot) % ratio, axis=0, keepdims=False)
        slots.append(jnp.transpose(got, (1, 0, 2)))
    mirror = jnp.concatenate(slots, axis=0)

    samples_shape = (1, 1, samples)
    src_depth = levels[0].reshape(samples_shape)
    rcv_depth = levels[1].reshape(samples_shape)
    src_ends = jnp.stack([src_index == 0, src_index == src_count - 1]).astype(jnp.int32)
    rcv_ends = jnp.stack([rcv_index == 0, rcv_index == rcv_count - 1]).astype(jnp.int32)

    merged_wide = extend(merged, "src", 0, SRC_HALO)
    mirror_wide = extend(mirror, "src", 0, SRC_HALO)
    coeff = lift_stage("fwd", (merged_wide, mirror_wide), src_ends, src_depth, SRC_HALO, row_count)

    wide = jnp.moveaxis(extend(coeff, "rcv", 1, RCV_HALO), 1, 0)
    turned = lift_stage(
        "both", (thresholds.reshape(samples_shape), wide), rcv_ends, rcv_depth, RCV_HALO, col_count
    )
    coeff = jnp.moveaxis(turned, 0, 1)

    wide = extend(coeff, "src", 0, SRC_HALO)
    return lift_stage("inv", (wide,), src_ends, src_depth, SRC_HALO, row_count)

def solution(mesh):
    return jax.shard_map(
        body,
        mesh=mesh,
        in_specs=(P("src", "rcv", None), P("src", "rcv", None), P(), P(), P()),
        out_specs=P("src", "rcv", None),
        check_vma=False,
    )
```

```python
import functools

import jax
import jax.numpy as jnp
from jax import lax
from jax.sharding import PartitionSpec as P
from jax.experimental import pallas as pl
from jax.experimental.pallas import tpu as pltpu

LEVELS = 3
SRC_HALO = 16
RCV_HALO = 24


def split_pairs(field, stride):
    length = field.shape[0]
    shaped = field.reshape((length // (2 * stride), 2, stride) + field.shape[1:])
    return (shaped, shaped[:, :, 0])


def join_pairs(shaped, new_pairs, field):
    joined = jnp.concatenate([new_pairs[:, :, None], shaped[:, :, 1:]], axis=2)
    return joined.reshape(field.shape)


def forward_core(pair_rows, first, last):
    even_part = pair_rows[:, 0]
    odd_part = pair_rows[:, 1]
    next_even = jnp.concatenate([even_part[1:], even_part[-1:]], axis=0)
    next_even = jnp.where(last, even_part, next_even)
    detail = odd_part - 0.5 * (even_part + next_even)
    prev_detail = jnp.concatenate([detail[:1], detail[:-1]], axis=0)
    prev_detail = jnp.where(first, detail, prev_detail)
    smooth = even_part + 0.25 * (prev_detail + detail)
    return jnp.stack([smooth, detail], axis=1)


def inverse_core(pair_rows, first, last):
    smooth = pair_rows[:, 0]
    detail = pair_rows[:, 1]
    prev_detail = jnp.concatenate([detail[:1], detail[:-1]], axis=0)
    prev_detail = jnp.where(first, detail, prev_detail)
    even_part = smooth - 0.25 * (prev_detail + detail)
    next_even = jnp.concatenate([even_part[1:], even_part[-1:]], axis=0)
    next_even = jnp.where(last, even_part, next_even)
    odd_part = detail + 0.5 * (even_part + next_even)
    return jnp.stack([even_part, odd_part], axis=1)


def level(field, stride, enabled, forward, width, length, is_first, is_last):
    shaped, pair_rows = split_pairs(field, stride)
    pair_ids = jnp.arange(pair_rows.shape[0], dtype=jnp.int32).reshape(
        (-1,) + (1,) * (pair_rows.ndim - 2)
    )
    first = is_first & (pair_ids == width // (2 * stride))
    last = is_last & (pair_ids == (width + length) // (2 * stride) - 1)
    core = forward_core if forward else inverse_core
    new_pairs = core(pair_rows, first, last)
    return jnp.where(enabled, join_pairs(shaped, new_pairs, field), field)


PAD = 8


def _lift_level(work, stride, enabled, forward, width, length, ends):
    rows = work.shape[0] - 2 * PAD
    pairs = rows // (2 * stride)
    step = 2 * stride
    pair_ids = lax.broadcasted_iota(jnp.int32, (pairs,) + work.shape[1:], 0)
    first = (pair_ids == width // step) & (ends[0] != 0)
    last = (pair_ids == (width + length) // step - 1) & (ends[1] != 0)
    evens = pl.ds(PAD, pairs, stride=step)
    odds = pl.ds(PAD + stride, pairs, stride=step)
    next_evens = pl.ds(PAD + step, pairs, stride=step)
    prev_odds = pl.ds(PAD - stride, pairs, stride=step)
    if forward:
        even_part = work[evens]
        odd_part = work[odds]
        next_even = jnp.where(last, even_part, work[next_evens])
        detail = odd_part - 0.5 * (even_part + next_even)
        work[odds] = jnp.where(enabled, detail, odd_part)
        prev_detail = jnp.where(first, detail, work[prev_odds])
        smooth = even_part + 0.25 * (prev_detail + detail)
        work[evens] = jnp.where(enabled, smooth, even_part)
    else:
        smooth = work[evens]
        detail = work[odds]
        prev_detail = jnp.where(first, detail, work[prev_odds])
        even_part = smooth - 0.25 * (prev_detail + detail)
        work[evens] = jnp.where(enabled, even_part, smooth)
        next_even = jnp.where(last, even_part, work[next_evens])
        odd_part = detail + 0.5 * (even_part + next_even)
        work[odds] = jnp.where(enabled, odd_part, detail)


def _stage_kernel(*refs, kind, width, length, out_from, out_rows):
    if kind == "fwd":
        ends_ref, depth_ref, left_ref, right_ref, out_ref, work = refs
    elif kind == "both":
        ends_ref, depth_ref, thr_ref, in_ref, out_ref, work = refs
    else:
        ends_ref, depth_ref, in_ref, out_ref, work = refs
    rows = work.shape[0] - 2 * PAD
    ends = (ends_ref[0], ends_ref[1])
    depth = depth_ref[...]
    if kind == "fwd":
        work[PAD : PAD + rows] = 0.5 * (
            left_ref[...].astype(jnp.float32) + right_ref[...].astype(jnp.float32)
        )
    else:
        work[PAD : PAD + rows] = in_ref[...]
    if kind != "inv":
        for depth_index in range(LEVELS):
            _lift_level(work, 2**depth_index, depth > depth_index, True, width, length, ends)
    if kind == "both":
        field = work[PAD : PAD + rows]
        thr = thr_ref[...]
        work[PAD : PAD + rows] = field - jnp.clip(field, -thr, thr)
    if kind != "fwd":
        for depth_index in reversed(range(LEVELS)):
            _lift_level(work, 2**depth_index, depth > depth_index, False, width, length, ends)
    out_ref[...] = work[PAD + out_from : PAD + out_from + out_rows]


def lift_stage(kind, operands, ends, depth, width, length, out_from, out_rows):
    rows, cols, samples = operands[-1].shape
    kernel = functools.partial(
        _stage_kernel, kind=kind, width=width, length=length, out_from=out_from, out_rows=out_rows
    )
    smem = pl.BlockSpec(memory_space=pltpu.SMEM)
    vmem = pl.BlockSpec(memory_space=pltpu.VMEM)
    return pl.pallas_call(
        kernel,
        out_shape=jax.ShapeDtypeStruct((out_rows, cols, samples), jnp.float32),
        in_specs=[smem] + [vmem] * (1 + len(operands)),
        out_specs=vmem,
        scratch_shapes=[pltpu.VMEM((rows + 2 * PAD, cols, samples), jnp.float32)],
    )(ends, depth, *operands)


def extend(cells, axis_name, dim, width):
    count = lax.axis_size(axis_name)
    length = cells.shape[dim]
    head = lax.slice_in_dim(cells, 0, width, axis=dim)
    tail = lax.slice_in_dim(cells, length - width, length, axis=dim)
    from_left = lax.ppermute(tail, axis_name, [(i, i + 1) for i in range(count - 1)])
    from_right = lax.ppermute(head, axis_name, [(i + 1, i) for i in range(count - 1)])
    return jnp.concatenate([from_left, cells, from_right], axis=dim)


def body(observed, estimate, acquired, levels, thresholds):
    src_count = lax.axis_size("src")
    rcv_count = lax.axis_size("rcv")
    src_index = lax.axis_index("src")
    rcv_index = lax.axis_index("rcv")
    row_count, col_count, samples = observed.shape
    extent = row_count * src_count
    blocks = acquired.shape[0]
    block_size = extent // blocks
    block_ids = jnp.arange(blocks, dtype=jnp.int32)
    row_ids = src_index * row_count + jnp.arange(row_count, dtype=jnp.int32)
    col_ids = rcv_index * col_count + jnp.arange(col_count, dtype=jnp.int32)
    pick_rows = (row_ids[:, None] // block_size == block_ids[None, :]).astype(jnp.float32)
    pick_cols = (col_ids[:, None] // block_size == block_ids[None, :]).astype(jnp.float32)
    row_mask = jnp.dot(pick_rows, acquired.astype(jnp.float32), precision=lax.Precision.HIGHEST)
    local_mask = jnp.dot(row_mask, pick_cols.T, precision=lax.Precision.HIGHEST)
    est_float = estimate.astype(jnp.float32)
    merged = (
        est_float + local_mask[:, :, None] * (observed.astype(jnp.float32) - est_float)
    ).astype(jnp.bfloat16)

    assert rcv_count == 2 * src_count and row_count == 2 * col_count
    mirror_halo = col_count
    pieces = merged.reshape(2, col_count, col_count, samples)
    own_part = rcv_index % 2
    everyone = ("src", "rcv")
    received = {}
    for c in range(2):
        for r in range(2):
            perm = []
            for a in range(src_count):
                for b in range(rcv_count):
                    q = (b + 1) % 2 + 2 * r
                    if (b + 1 - q) % 2 == 0 and 0 <= (b + 1 - q) // 2 < src_count:
                        target = ((b + 1 - q) // 2) * rcv_count + 2 * a + (b + c) % 2
                        perm.append((a * rcv_count + b, target))
            send = jnp.where((own_part + c) % 2 == 0, pieces[0], pieces[1])
            received[c, r] = lax.ppermute(send, everyone, perm)
    slots = []
    for q in range(4):
        even_c = (1 - q % 2) % 2
        got = jnp.where(own_part == 0, received[even_c, q // 2], received[1 - even_c, q // 2])
        slots.append(jnp.transpose(got, (1, 0, 2)))
    mirror_wide = jnp.concatenate(slots, axis=0)
    merged_wide = extend(merged, "src", 0, mirror_halo)

    samples_shape = (1, 1, samples)
    src_depth = levels[0].reshape(samples_shape)
    rcv_depth = levels[1].reshape(samples_shape)
    src_ends = jnp.stack([src_index == 0, src_index == src_count - 1]).astype(jnp.int32)
    rcv_ends = jnp.stack([rcv_index == 0, rcv_index == rcv_count - 1]).astype(jnp.int32)

    coeff = lift_stage(
        "fwd", (merged_wide, mirror_wide), src_ends, src_depth, mirror_halo, row_count,
        mirror_halo - SRC_HALO, row_count + 2 * SRC_HALO,
    )

    wide = jnp.moveaxis(extend(coeff, "rcv", 1, RCV_HALO), 1, 0)
    turned = lift_stage(
        "both", (thresholds.reshape(samples_shape), wide), rcv_ends, rcv_depth, RCV_HALO, col_count,
        RCV_HALO, col_count,
    )
    coeff = jnp.moveaxis(turned, 0, 1)
    return lift_stage("inv", (coeff,), src_ends, src_depth, SRC_HALO, row_count, SRC_HALO, row_count)

def solution(mesh):
    return jax.shard_map(
        body,
        mesh=mesh,
        in_specs=(P("src", "rcv", None), P("src", "rcv", None), P(), P(), P()),
        out_specs=P("src", "rcv", None),
        check_vma=False,
    )
```

```python
import functools

import jax
import jax.numpy as jnp
from jax import lax
from jax.sharding import PartitionSpec as P
from jax.experimental import pallas as pl
from jax.experimental.pallas import tpu as pltpu

LEVELS = 3
SRC_HALO = 16
RCV_HALO = 24


def split_pairs(field, stride):
    length = field.shape[0]
    shaped = field.reshape((length // (2 * stride), 2, stride) + field.shape[1:])
    return (shaped, shaped[:, :, 0])


def join_pairs(shaped, new_pairs, field):
    joined = jnp.concatenate([new_pairs[:, :, None], shaped[:, :, 1:]], axis=2)
    return joined.reshape(field.shape)


def forward_core(pair_rows, first, last):
    even_part = pair_rows[:, 0]
    odd_part = pair_rows[:, 1]
    next_even = jnp.concatenate([even_part[1:], even_part[-1:]], axis=0)
    next_even = jnp.where(last, even_part, next_even)
    detail = odd_part - 0.5 * (even_part + next_even)
    prev_detail = jnp.concatenate([detail[:1], detail[:-1]], axis=0)
    prev_detail = jnp.where(first, detail, prev_detail)
    smooth = even_part + 0.25 * (prev_detail + detail)
    return jnp.stack([smooth, detail], axis=1)


def inverse_core(pair_rows, first, last):
    smooth = pair_rows[:, 0]
    detail = pair_rows[:, 1]
    prev_detail = jnp.concatenate([detail[:1], detail[:-1]], axis=0)
    prev_detail = jnp.where(first, detail, prev_detail)
    even_part = smooth - 0.25 * (prev_detail + detail)
    next_even = jnp.concatenate([even_part[1:], even_part[-1:]], axis=0)
    next_even = jnp.where(last, even_part, next_even)
    odd_part = detail + 0.5 * (even_part + next_even)
    return jnp.stack([even_part, odd_part], axis=1)


def level(field, stride, enabled, forward, width, length, is_first, is_last):
    shaped, pair_rows = split_pairs(field, stride)
    pair_ids = jnp.arange(pair_rows.shape[0], dtype=jnp.int32).reshape(
        (-1,) + (1,) * (pair_rows.ndim - 2)
    )
    first = is_first & (pair_ids == width // (2 * stride))
    last = is_last & (pair_ids == (width + length) // (2 * stride) - 1)
    core = forward_core if forward else inverse_core
    new_pairs = core(pair_rows, first, last)
    return jnp.where(enabled, join_pairs(shaped, new_pairs, field), field)


PAD = 8


def _lift_level(work, stride, enabled, forward, width, length, ends):
    rows = work.shape[0] - 2 * PAD
    pairs = rows // (2 * stride)
    step = 2 * stride
    pair_ids = lax.broadcasted_iota(jnp.int32, (pairs,) + work.shape[1:], 0)
    first = (pair_ids == width // step) & (ends[0] != 0)
    last = (pair_ids == (width + length) // step - 1) & (ends[1] != 0)
    evens = pl.ds(PAD, pairs, stride=step)
    odds = pl.ds(PAD + stride, pairs, stride=step)
    next_evens = pl.ds(PAD + step, pairs, stride=step)
    prev_odds = pl.ds(PAD - stride, pairs, stride=step)
    if forward:
        even_part = work[evens]
        odd_part = work[odds]
        next_even = jnp.where(last, even_part, work[next_evens])
        detail = odd_part - 0.5 * (even_part + next_even)
        work[odds] = jnp.where(enabled, detail, odd_part)
        prev_detail = jnp.where(first, detail, work[prev_odds])
        smooth = even_part + 0.25 * (prev_detail + detail)
        work[evens] = jnp.where(enabled, smooth, even_part)
    else:
        smooth = work[evens]
        detail = work[odds]
        prev_detail = jnp.where(first, detail, work[prev_odds])
        even_part = smooth - 0.25 * (prev_detail + detail)
        work[evens] = jnp.where(enabled, even_part, smooth)
        next_even = jnp.where(last, even_part, work[next_evens])
        odd_part = detail + 0.5 * (even_part + next_even)
        work[odds] = jnp.where(enabled, odd_part, detail)


def _stage_kernel(*refs, kind, width, length, out_from, out_rows):
    if kind == "fwd":
        ends_ref, depth_ref, left_ref, right_ref, out_ref, work = refs
    elif kind == "both":
        ends_ref, depth_ref, thr_ref, in_ref, out_ref, work = refs
    else:
        ends_ref, depth_ref, in_ref, out_ref, work = refs
    rows = work.shape[0] - 2 * PAD
    ends = (ends_ref[0], ends_ref[1])
    depth = depth_ref[...]
    if kind == "fwd":
        work[PAD : PAD + rows] = 0.5 * (
            left_ref[...].astype(jnp.float32) + right_ref[...].astype(jnp.float32)
        )
    else:
        work[PAD : PAD + rows] = in_ref[...]
    if kind != "inv":
        for depth_index in range(LEVELS):
            _lift_level(work, 2**depth_index, depth > depth_index, True, width, length, ends)
    if kind == "both":
        field = work[PAD : PAD + rows]
        thr = thr_ref[...]
        work[PAD : PAD + rows] = field - jnp.clip(field, -thr, thr)
    if kind != "fwd":
        for depth_index in reversed(range(LEVELS)):
            _lift_level(work, 2**depth_index, depth > depth_index, False, width, length, ends)
    out_ref[...] = work[PAD + out_from : PAD + out_from + out_rows]


def lift_stage(kind, operands, ends, depth, width, length, out_from, out_rows):
    rows, cols, samples = operands[-1].shape
    kernel = functools.partial(
        _stage_kernel, kind=kind, width=width, length=length, out_from=out_from, out_rows=out_rows
    )
    smem = pl.BlockSpec(memory_space=pltpu.SMEM)
    vmem = pl.BlockSpec(memory_space=pltpu.VMEM)
    return pl.pallas_call(
        kernel,
        out_shape=jax.ShapeDtypeStruct((out_rows, cols, samples), jnp.float32),
        in_specs=[smem] + [vmem] * (1 + len(operands)),
        out_specs=vmem,
        scratch_shapes=[pltpu.VMEM((rows + 2 * PAD, cols, samples), jnp.float32)],
    )(ends, depth, *operands)


def extend(cells, axis_name, dim, width):
    count = lax.axis_size(axis_name)
    length = cells.shape[dim]
    head = lax.slice_in_dim(cells, 0, width, axis=dim)
    tail = lax.slice_in_dim(cells, length - width, length, axis=dim)
    from_left = lax.ppermute(tail, axis_name, [(i, i + 1) for i in range(count - 1)])
    from_right = lax.ppermute(head, axis_name, [(i + 1, i) for i in range(count - 1)])
    return jnp.concatenate([from_left, cells, from_right], axis=dim)


def body(observed, estimate, acquired, levels, thresholds):
    src_count = lax.axis_size("src")
    rcv_count = lax.axis_size("rcv")
    src_index = lax.axis_index("src")
    rcv_index = lax.axis_index("rcv")
    row_count, col_count, samples = observed.shape
    extent = row_count * src_count
    blocks = acquired.shape[0]
    block_size = extent // blocks
    block_ids = jnp.arange(blocks, dtype=jnp.int32)
    row_ids = src_index * row_count + jnp.arange(row_count, dtype=jnp.int32)
    col_ids = rcv_index * col_count + jnp.arange(col_count, dtype=jnp.int32)
    pick_rows = (row_ids[:, None] // block_size == block_ids[None, :]).astype(jnp.float32)
    pick_cols = (col_ids[:, None] // block_size == block_ids[None, :]).astype(jnp.float32)
    row_mask = jnp.dot(pick_rows, acquired.astype(jnp.float32), precision=lax.Precision.HIGHEST)
    local_mask = jnp.dot(row_mask, pick_cols.T, precision=lax.Precision.HIGHEST)
    est_float = estimate.astype(jnp.float32)
    merged = (
        est_float + local_mask[:, :, None] * (observed.astype(jnp.float32) - est_float)
    ).astype(jnp.bfloat16)

    ratio = rcv_count // src_count
    pieces = merged.reshape(ratio, col_count, col_count, samples)
    own_part = rcv_index % ratio
    received = []
    for shift in range(ratio):
        perm = []
        for a in range(src_count):
            for b in range(rcv_count):
                part = (b % ratio + shift) % ratio
                perm.append((a * rcv_count + b, (b // ratio) * rcv_count + a * ratio + part))
        send = lax.dynamic_index_in_dim(pieces, (own_part + shift) % ratio, axis=0, keepdims=False)
        received.append(lax.ppermute(send, ("src", "rcv"), perm))
    received = jnp.stack(received)
    slots = []
    for slot in range(ratio):
        got = lax.dynamic_index_in_dim(received, (own_part - slot) % ratio, axis=0, keepdims=False)
        slots.append(jnp.transpose(got, (1, 0, 2)))
    mirror = jnp.concatenate(slots, axis=0)
    mirror_halo = 2 * SRC_HALO
    mirror_wide = extend(mirror, "src", 0, mirror_halo)
    merged_wide = extend(merged, "src", 0, mirror_halo)

    samples_shape = (1, 1, samples)
    src_depth = levels[0].reshape(samples_shape)
    rcv_depth = levels[1].reshape(samples_shape)
    src_ends = jnp.stack([src_index == 0, src_index == src_count - 1]).astype(jnp.int32)
    rcv_ends = jnp.stack([rcv_index == 0, rcv_index == rcv_count - 1]).astype(jnp.int32)

    coeff = lift_stage(
        "fwd", (merged_wide, mirror_wide), src_ends, src_depth, mirror_halo, row_count,
        mirror_halo - SRC_HALO, row_count + 2 * SRC_HALO,
    )

    wide = jnp.moveaxis(extend(coeff, "rcv", 1, RCV_HALO), 1, 0)
    turned = lift_stage(
        "both", (thresholds.reshape(samples_shape), wide), rcv_ends, rcv_depth, RCV_HALO, col_count,
        RCV_HALO, col_count,
    )
    coeff = jnp.moveaxis(turned, 0, 1)
    return lift_stage("inv", (coeff,), src_ends, src_depth, SRC_HALO, row_count, SRC_HALO, row_count)

def solution(mesh):
    return jax.shard_map(
        body,
        mesh=mesh,
        in_specs=(P("src", "rcv", None), P("src", "rcv", None), P(), P(), P()),
        out_specs=P("src", "rcv", None),
        check_vma=False,
    )
```

```python
import functools

import jax
import jax.numpy as jnp
from jax import lax
from jax.sharding import PartitionSpec as P
from jax.experimental import pallas as pl
from jax.experimental.pallas import tpu as pltpu

LEVELS = 3
SRC_HALO = 16
RCV_HALO = 24


def split_pairs(field, stride):
    length = field.shape[0]
    shaped = field.reshape((length // (2 * stride), 2, stride) + field.shape[1:])
    return (shaped, shaped[:, :, 0])


def join_pairs(shaped, new_pairs, field):
    joined = jnp.concatenate([new_pairs[:, :, None], shaped[:, :, 1:]], axis=2)
    return joined.reshape(field.shape)


def forward_core(pair_rows, first, last):
    even_part = pair_rows[:, 0]
    odd_part = pair_rows[:, 1]
    next_even = jnp.concatenate([even_part[1:], even_part[-1:]], axis=0)
    next_even = jnp.where(last, even_part, next_even)
    detail = odd_part - 0.5 * (even_part + next_even)
    prev_detail = jnp.concatenate([detail[:1], detail[:-1]], axis=0)
    prev_detail = jnp.where(first, detail, prev_detail)
    smooth = even_part + 0.25 * (prev_detail + detail)
    return jnp.stack([smooth, detail], axis=1)


def inverse_core(pair_rows, first, last):
    smooth = pair_rows[:, 0]
    detail = pair_rows[:, 1]
    prev_detail = jnp.concatenate([detail[:1], detail[:-1]], axis=0)
    prev_detail = jnp.where(first, detail, prev_detail)
    even_part = smooth - 0.25 * (prev_detail + detail)
    next_even = jnp.concatenate([even_part[1:], even_part[-1:]], axis=0)
    next_even = jnp.where(last, even_part, next_even)
    odd_part = detail + 0.5 * (even_part + next_even)
    return jnp.stack([even_part, odd_part], axis=1)


def level(field, stride, enabled, forward, width, length, is_first, is_last):
    shaped, pair_rows = split_pairs(field, stride)
    pair_ids = jnp.arange(pair_rows.shape[0], dtype=jnp.int32).reshape(
        (-1,) + (1,) * (pair_rows.ndim - 2)
    )
    first = is_first & (pair_ids == width // (2 * stride))
    last = is_last & (pair_ids == (width + length) // (2 * stride) - 1)
    core = forward_core if forward else inverse_core
    new_pairs = core(pair_rows, first, last)
    return jnp.where(enabled, join_pairs(shaped, new_pairs, field), field)


PAD = 8


def _lift_level(work, stride, enabled, forward, width, length, ends, axis=0):
    rows = work.shape[axis] - 2 * PAD
    pairs = rows // (2 * stride)
    step = 2 * stride
    shape = list(work.shape)
    shape[axis] = pairs
    pair_ids = lax.broadcasted_iota(jnp.int32, tuple(shape), axis)
    first = (pair_ids == width // step) & (ends[0] != 0)
    last = (pair_ids == (width + length) // step - 1) & (ends[1] != 0)

    def at(start):
        window = pl.ds(start, pairs, stride=step)
        return (window,) if axis == 0 else (slice(None), window)

    evens = at(PAD)
    odds = at(PAD + stride)
    next_evens = at(PAD + step)
    prev_odds = at(PAD - stride)
    if forward:
        even_part = work[evens]
        odd_part = work[odds]
        next_even = jnp.where(last, even_part, work[next_evens])
        detail = odd_part - 0.5 * (even_part + next_even)
        work[odds] = jnp.where(enabled, detail, odd_part)
        prev_detail = jnp.where(first, detail, work[prev_odds])
        smooth = even_part + 0.25 * (prev_detail + detail)
        work[evens] = jnp.where(enabled, smooth, even_part)
    else:
        smooth = work[evens]
        detail = work[odds]
        prev_detail = jnp.where(first, detail, work[prev_odds])
        even_part = smooth - 0.25 * (prev_detail + detail)
        work[evens] = jnp.where(enabled, even_part, smooth)
        next_even = jnp.where(last, even_part, work[next_evens])
        odd_part = detail + 0.5 * (even_part + next_even)
        work[odds] = jnp.where(enabled, odd_part, detail)


def _rcv_kernel(ends_ref, depth_ref, thr_ref, left_ref, mid_ref, right_ref, out_ref, work, *, width):
    length = mid_ref.shape[1]
    ends = (ends_ref[0], ends_ref[1])
    depth = depth_ref[...]
    work[:, PAD : PAD + width] = left_ref[...]
    work[:, PAD + width : PAD + width + length] = mid_ref[...]
    work[:, PAD + width + length : PAD + 2 * width + length] = right_ref[...]
    for depth_index in range(LEVELS):
        _lift_level(work, 2**depth_index, depth > depth_index, True, width, length, ends, axis=1)
    field = work[:, PAD : PAD + 2 * width + length]
    thr = thr_ref[...]
    work[:, PAD : PAD + 2 * width + length] = field - jnp.clip(field, -thr, thr)
    for depth_index in reversed(range(LEVELS)):
        _lift_level(work, 2**depth_index, depth > depth_index, False, width, length, ends, axis=1)
    out_ref[...] = work[:, PAD + width : PAD + width + length]


def rcv_stage(left, mid, right, thr, ends, depth, width):
    rows, cols, samples = mid.shape
    smem = pl.BlockSpec(memory_space=pltpu.SMEM)
    vmem = pl.BlockSpec(memory_space=pltpu.VMEM)
    return pl.pallas_call(
        functools.partial(_rcv_kernel, width=width),
        out_shape=jax.ShapeDtypeStruct(mid.shape, jnp.float32),
        in_specs=[smem] + [vmem] * 5,
        out_specs=vmem,
        scratch_shapes=[pltpu.VMEM((rows, cols + 2 * width + 2 * PAD, samples), jnp.float32)],
    )(ends, depth, thr, left, mid, right)


def _stage_kernel(*refs, kind, width, length, out_from, out_rows):
    if kind == "fwd":
        ends_ref, depth_ref, terms_ref, out_ref, work = refs
    elif kind == "both":
        ends_ref, depth_ref, thr_ref, in_ref, out_ref, work = refs
    else:
        ends_ref, depth_ref, in_ref, out_ref, work = refs
    rows = work.shape[0] - 2 * PAD
    ends = (ends_ref[0], ends_ref[1])
    depth = depth_ref[...]
    if kind == "fwd":
        work[PAD : PAD + rows] = 0.5 * (
            terms_ref[:, 0].astype(jnp.float32) + terms_ref[:, 1].astype(jnp.float32)
        )
    else:
        work[PAD : PAD + rows] = in_ref[...]
    if kind != "inv":
        for depth_index in range(LEVELS):
            _lift_level(work, 2**depth_index, depth > depth_index, True, width, length, ends)
    if kind == "both":
        field = work[PAD : PAD + rows]
        thr = thr_ref[...]
        work[PAD : PAD + rows] = field - jnp.clip(field, -thr, thr)
    if kind != "fwd":
        for depth_index in reversed(range(LEVELS)):
            _lift_level(work, 2**depth_index, depth > depth_index, False, width, length, ends)
    out_ref[...] = work[PAD + out_from : PAD + out_from + out_rows]


def lift_stage(kind, operands, ends, depth, width, length, out_from, out_rows):
    rows = operands[-1].shape[0]
    cols, samples = operands[-1].shape[-2:]
    kernel = functools.partial(
        _stage_kernel, kind=kind, width=width, length=length, out_from=out_from, out_rows=out_rows
    )
    smem = pl.BlockSpec(memory_space=pltpu.SMEM)
    vmem = pl.BlockSpec(memory_space=pltpu.VMEM)
    return pl.pallas_call(
        kernel,
        out_shape=jax.ShapeDtypeStruct((out_rows, cols, samples), jnp.float32),
        in_specs=[smem] + [vmem] * (1 + len(operands)),
        out_specs=vmem,
        scratch_shapes=[pltpu.VMEM((rows + 2 * PAD, cols, samples), jnp.float32)],
    )(ends, depth, *operands)


def halos(cells, axis_name, dim, width):
    count = lax.axis_size(axis_name)
    length = cells.shape[dim]
    head = lax.slice_in_dim(cells, 0, width, axis=dim)
    tail = lax.slice_in_dim(cells, length - width, length, axis=dim)
    from_left = lax.ppermute(tail, axis_name, [(i, i + 1) for i in range(count - 1)])
    from_right = lax.ppermute(head, axis_name, [(i + 1, i) for i in range(count - 1)])
    return from_left, from_right


def extend(cells, axis_name, dim, width):
    from_left, from_right = halos(cells, axis_name, dim, width)
    return jnp.concatenate([from_left, cells, from_right], axis=dim)


def body(observed, estimate, acquired, levels, thresholds):
    src_count = lax.axis_size("src")
    rcv_count = lax.axis_size("rcv")
    src_index = lax.axis_index("src")
    rcv_index = lax.axis_index("rcv")
    row_count, col_count, samples = observed.shape
    extent = row_count * src_count
    blocks = acquired.shape[0]
    block_size = extent // blocks
    block_ids = jnp.arange(blocks, dtype=jnp.int32)
    row_ids = src_index * row_count + jnp.arange(row_count, dtype=jnp.int32)
    col_ids = rcv_index * col_count + jnp.arange(col_count, dtype=jnp.int32)
    pick_rows = (row_ids[:, None] // block_size == block_ids[None, :]).astype(jnp.float32)
    pick_cols = (col_ids[:, None] // block_size == block_ids[None, :]).astype(jnp.float32)
    row_mask = jnp.dot(pick_rows, acquired.astype(jnp.float32), precision=lax.Precision.HIGHEST)
    local_mask = jnp.dot(row_mask, pick_cols.T, precision=lax.Precision.HIGHEST)
    est_float = estimate.astype(jnp.float32)
    merged = (
        est_float + local_mask[:, :, None] * (observed.astype(jnp.float32) - est_float)
    ).astype(jnp.bfloat16)

    ratio = rcv_count // src_count
    pieces = merged.reshape(ratio, col_count, col_count, samples)
    own_part = rcv_index % ratio
    received = []
    for shift in range(ratio):
        perm = []
        for a in range(src_count):
            for b in range(rcv_count):
                part = (b % ratio + shift) % ratio
                perm.append((a * rcv_count + b, (b // ratio) * rcv_count + a * ratio + part))
        send = lax.dynamic_index_in_dim(pieces, (own_part + shift) % ratio, axis=0, keepdims=False)
        received.append(lax.ppermute(send, ("src", "rcv"), perm))
    received = jnp.stack(received)
    slots = []
    for slot in range(ratio):
        got = lax.dynamic_index_in_dim(received, (own_part - slot) % ratio, axis=0, keepdims=False)
        slots.append(jnp.transpose(got, (1, 0, 2)))
    mirror = jnp.concatenate(slots, axis=0)
    mirror_halo = 2 * SRC_HALO
    terms = extend(jnp.stack([merged, mirror], axis=1), "src", 0, mirror_halo)

    samples_shape = (1, 1, samples)
    src_depth = levels[0].reshape(samples_shape)
    rcv_depth = levels[1].reshape(samples_shape)
    src_ends = jnp.stack([src_index == 0, src_index == src_count - 1]).astype(jnp.int32)
    rcv_ends = jnp.stack([rcv_index == 0, rcv_index == rcv_count - 1]).astype(jnp.int32)

    coeff = lift_stage(
        "fwd", (terms,), src_ends, src_depth, mirror_halo, row_count,
        mirror_halo - SRC_HALO, row_count + 2 * SRC_HALO,
    )

    from_left, from_right = halos(coeff, "rcv", 1, RCV_HALO)
    coeff = rcv_stage(
        from_left, coeff, from_right, thresholds.reshape(samples_shape), rcv_ends, rcv_depth, RCV_HALO
    )
    return lift_stage("inv", (coeff,), src_ends, src_depth, SRC_HALO, row_count, SRC_HALO, row_count)

def solution(mesh):
    return jax.shard_map(
        body,
        mesh=mesh,
        in_specs=(P("src", "rcv", None), P("src", "rcv", None), P(), P(), P()),
        out_specs=P("src", "rcv", None),
        check_vma=False,
    )
```

```python
import functools

import jax
import jax.numpy as jnp
from jax import lax
from jax.sharding import PartitionSpec as P
from jax.experimental import pallas as pl
from jax.experimental.pallas import tpu as pltpu

LEVELS = 3
SRC_HALO = 16
RCV_HALO = 24
MIRROR_SPLIT = 4


def split_pairs(field, stride):
    length = field.shape[0]
    shaped = field.reshape((length // (2 * stride), 2, stride) + field.shape[1:])
    return (shaped, shaped[:, :, 0])


def join_pairs(shaped, new_pairs, field):
    joined = jnp.concatenate([new_pairs[:, :, None], shaped[:, :, 1:]], axis=2)
    return joined.reshape(field.shape)


def forward_core(pair_rows, first, last):
    even_part = pair_rows[:, 0]
    odd_part = pair_rows[:, 1]
    next_even = jnp.concatenate([even_part[1:], even_part[-1:]], axis=0)
    next_even = jnp.where(last, even_part, next_even)
    detail = odd_part - 0.5 * (even_part + next_even)
    prev_detail = jnp.concatenate([detail[:1], detail[:-1]], axis=0)
    prev_detail = jnp.where(first, detail, prev_detail)
    smooth = even_part + 0.25 * (prev_detail + detail)
    return jnp.stack([smooth, detail], axis=1)


def inverse_core(pair_rows, first, last):
    smooth = pair_rows[:, 0]
    detail = pair_rows[:, 1]
    prev_detail = jnp.concatenate([detail[:1], detail[:-1]], axis=0)
    prev_detail = jnp.where(first, detail, prev_detail)
    even_part = smooth - 0.25 * (prev_detail + detail)
    next_even = jnp.concatenate([even_part[1:], even_part[-1:]], axis=0)
    next_even = jnp.where(last, even_part, next_even)
    odd_part = detail + 0.5 * (even_part + next_even)
    return jnp.stack([even_part, odd_part], axis=1)


def level(field, stride, enabled, forward, width, length, is_first, is_last):
    shaped, pair_rows = split_pairs(field, stride)
    pair_ids = jnp.arange(pair_rows.shape[0], dtype=jnp.int32).reshape(
        (-1,) + (1,) * (pair_rows.ndim - 2)
    )
    first = is_first & (pair_ids == width // (2 * stride))
    last = is_last & (pair_ids == (width + length) // (2 * stride) - 1)
    core = forward_core if forward else inverse_core
    new_pairs = core(pair_rows, first, last)
    return jnp.where(enabled, join_pairs(shaped, new_pairs, field), field)


PAD = 8


def _lift_level(work, stride, enabled, forward, width, length, ends, axis=0):
    rows = work.shape[axis] - 2 * PAD
    pairs = rows // (2 * stride)
    step = 2 * stride
    shape = list(work.shape)
    shape[axis] = pairs
    pair_ids = lax.broadcasted_iota(jnp.int32, tuple(shape), axis)
    first = (pair_ids == width // step) & (ends[0] != 0)
    last = (pair_ids == (width + length) // step - 1) & (ends[1] != 0)

    def at(start):
        window = pl.ds(start, pairs, stride=step)
        return (window,) if axis == 0 else (slice(None), window)

    evens = at(PAD)
    odds = at(PAD + stride)
    next_evens = at(PAD + step)
    prev_odds = at(PAD - stride)
    if forward:
        even_part = work[evens]
        odd_part = work[odds]
        next_even = jnp.where(last, even_part, work[next_evens])
        detail = odd_part - 0.5 * (even_part + next_even)
        work[odds] = jnp.where(enabled, detail, odd_part)
        prev_detail = jnp.where(first, detail, work[prev_odds])
        smooth = even_part + 0.25 * (prev_detail + detail)
        work[evens] = jnp.where(enabled, smooth, even_part)
    else:
        smooth = work[evens]
        detail = work[odds]
        prev_detail = jnp.where(first, detail, work[prev_odds])
        even_part = smooth - 0.25 * (prev_detail + detail)
        work[evens] = jnp.where(enabled, even_part, smooth)
        next_even = jnp.where(last, even_part, work[next_evens])
        odd_part = detail + 0.5 * (even_part + next_even)
        work[odds] = jnp.where(enabled, odd_part, detail)


def _rcv_kernel(ends_ref, depth_ref, thr_ref, left_ref, mid_ref, right_ref, out_ref, work, *, width):
    length = mid_ref.shape[1]
    ends = (ends_ref[0], ends_ref[1])
    depth = depth_ref[...]
    work[:, PAD : PAD + width] = left_ref[...]
    work[:, PAD + width : PAD + width + length] = mid_ref[...]
    work[:, PAD + width + length : PAD + 2 * width + length] = right_ref[...]
    for depth_index in range(LEVELS):
        _lift_level(work, 2**depth_index, depth > depth_index, True, width, length, ends, axis=1)
    field = work[:, PAD : PAD + 2 * width + length]
    thr = thr_ref[...]
    work[:, PAD : PAD + 2 * width + length] = field - jnp.clip(field, -thr, thr)
    for depth_index in reversed(range(LEVELS)):
        _lift_level(work, 2**depth_index, depth > depth_index, False, width, length, ends, axis=1)
    out_ref[...] = work[:, PAD + width : PAD + width + length]


def rcv_stage(left, mid, right, thr, ends, depth, width):
    rows, cols, samples = mid.shape
    smem = pl.BlockSpec(memory_space=pltpu.SMEM)
    vmem = pl.BlockSpec(memory_space=pltpu.VMEM)
    return pl.pallas_call(
        functools.partial(_rcv_kernel, width=width),
        out_shape=jax.ShapeDtypeStruct(mid.shape, jnp.float32),
        in_specs=[smem] + [vmem] * 5,
        out_specs=vmem,
        scratch_shapes=[pltpu.VMEM((rows, cols + 2 * width + 2 * PAD, samples), jnp.float32)],
    )(ends, depth, thr, left, mid, right)


def _stage_kernel(*refs, kind, width, length, out_from, out_rows):
    if kind == "fwd":
        ends_ref, depth_ref, terms_ref, out_ref, work = refs
    elif kind == "both":
        ends_ref, depth_ref, thr_ref, in_ref, out_ref, work = refs
    else:
        ends_ref, depth_ref, in_ref, out_ref, work = refs
    rows = work.shape[0] - 2 * PAD
    ends = (ends_ref[0], ends_ref[1])
    depth = depth_ref[...]
    if kind == "fwd":
        work[PAD : PAD + rows] = 0.5 * (
            terms_ref[:, 0].astype(jnp.float32) + terms_ref[:, 1].astype(jnp.float32)
        )
    else:
        work[PAD : PAD + rows] = in_ref[...]
    if kind != "inv":
        for depth_index in range(LEVELS):
            _lift_level(work, 2**depth_index, depth > depth_index, True, width, length, ends)
    if kind == "both":
        field = work[PAD : PAD + rows]
        thr = thr_ref[...]
        work[PAD : PAD + rows] = field - jnp.clip(field, -thr, thr)
    if kind != "fwd":
        for depth_index in reversed(range(LEVELS)):
            _lift_level(work, 2**depth_index, depth > depth_index, False, width, length, ends)
    out_ref[...] = work[PAD + out_from : PAD + out_from + out_rows]


def lift_stage(kind, operands, ends, depth, width, length, out_from, out_rows):
    rows = operands[-1].shape[0]
    cols, samples = operands[-1].shape[-2:]
    kernel = functools.partial(
        _stage_kernel, kind=kind, width=width, length=length, out_from=out_from, out_rows=out_rows
    )
    smem = pl.BlockSpec(memory_space=pltpu.SMEM)
    vmem = pl.BlockSpec(memory_space=pltpu.VMEM)
    return pl.pallas_call(
        kernel,
        out_shape=jax.ShapeDtypeStruct((out_rows, cols, samples), jnp.float32),
        in_specs=[smem] + [vmem] * (1 + len(operands)),
        out_specs=vmem,
        scratch_shapes=[pltpu.VMEM((rows + 2 * PAD, cols, samples), jnp.float32)],
    )(ends, depth, *operands)


def halos(cells, axis_name, dim, width):
    count = lax.axis_size(axis_name)
    length = cells.shape[dim]
    head = lax.slice_in_dim(cells, 0, width, axis=dim)
    tail = lax.slice_in_dim(cells, length - width, length, axis=dim)
    from_left = lax.ppermute(tail, axis_name, [(i, i + 1) for i in range(count - 1)])
    from_right = lax.ppermute(head, axis_name, [(i + 1, i) for i in range(count - 1)])
    return from_left, from_right


def extend(cells, axis_name, dim, width):
    from_left, from_right = halos(cells, axis_name, dim, width)
    return jnp.concatenate([from_left, cells, from_right], axis=dim)


def body(observed, estimate, acquired, levels, thresholds):
    src_count = lax.axis_size("src")
    rcv_count = lax.axis_size("rcv")
    src_index = lax.axis_index("src")
    rcv_index = lax.axis_index("rcv")
    row_count, col_count, samples = observed.shape
    extent = row_count * src_count
    blocks = acquired.shape[0]
    block_size = extent // blocks
    block_ids = jnp.arange(blocks, dtype=jnp.int32)
    row_ids = src_index * row_count + jnp.arange(row_count, dtype=jnp.int32)
    col_ids = rcv_index * col_count + jnp.arange(col_count, dtype=jnp.int32)
    pick_rows = (row_ids[:, None] // block_size == block_ids[None, :]).astype(jnp.float32)
    pick_cols = (col_ids[:, None] // block_size == block_ids[None, :]).astype(jnp.float32)
    row_mask = jnp.dot(pick_rows, acquired.astype(jnp.float32), precision=lax.Precision.HIGHEST)
    local_mask = jnp.dot(row_mask, pick_cols.T, precision=lax.Precision.HIGHEST)
    est_float = estimate.astype(jnp.float32)
    merged = (
        est_float + local_mask[:, :, None] * (observed.astype(jnp.float32) - est_float)
    ).astype(jnp.bfloat16)

    ratio = rcv_count // src_count
    pieces = merged.reshape(ratio, col_count, col_count, samples)
    own_part = rcv_index % ratio
    received = []
    for shift in range(ratio):
        perm = []
        for a in range(src_count):
            for b in range(rcv_count):
                part = (b % ratio + shift) % ratio
                perm.append((a * rcv_count + b, (b // ratio) * rcv_count + a * ratio + part))
        send = lax.dynamic_index_in_dim(pieces, (own_part + shift) % ratio, axis=0, keepdims=False)
        chunk = samples // MIRROR_SPLIT
        received.append(
            jnp.concatenate(
                [
                    lax.ppermute(send[:, :, k * chunk : (k + 1) * chunk], ("src", "rcv"), perm)
                    for k in range(MIRROR_SPLIT)
                ],
                axis=2,
            )
        )
    received = jnp.stack(received)
    slots = []
    for slot in range(ratio):
        got = lax.dynamic_index_in_dim(received, (own_part - slot) % ratio, axis=0, keepdims=False)
        slots.append(jnp.transpose(got, (1, 0, 2)))
    mirror = jnp.concatenate(slots, axis=0)
    mirror_halo = 2 * SRC_HALO
    terms = extend(jnp.stack([merged, mirror], axis=1), "src", 0, mirror_halo)

    samples_shape = (1, 1, samples)
    src_depth = levels[0].reshape(samples_shape)
    rcv_depth = levels[1].reshape(samples_shape)
    src_ends = jnp.stack([src_index == 0, src_index == src_count - 1]).astype(jnp.int32)
    rcv_ends = jnp.stack([rcv_index == 0, rcv_index == rcv_count - 1]).astype(jnp.int32)

    coeff = lift_stage(
        "fwd", (terms,), src_ends, src_depth, mirror_halo, row_count,
        mirror_halo - SRC_HALO, row_count + 2 * SRC_HALO,
    )

    from_left, from_right = halos(coeff, "rcv", 1, RCV_HALO)
    coeff = rcv_stage(
        from_left, coeff, from_right, thresholds.reshape(samples_shape), rcv_ends, rcv_depth, RCV_HALO
    )
    return lift_stage("inv", (coeff,), src_ends, src_depth, SRC_HALO, row_count, SRC_HALO, row_count)

def solution(mesh):
    return jax.shard_map(
        body,
        mesh=mesh,
        in_specs=(P("src", "rcv", None), P("src", "rcv", None), P(), P(), P()),
        out_specs=P("src", "rcv", None),
        check_vma=False,
    )
```

```python
import functools

import jax
import jax.numpy as jnp
from jax import lax
from jax.sharding import PartitionSpec as P
from jax.experimental import pallas as pl
from jax.experimental.pallas import tpu as pltpu

LEVELS = 3
SRC_HALO = 16
RCV_HALO = 24


def split_pairs(field, stride):
    length = field.shape[0]
    shaped = field.reshape((length // (2 * stride), 2, stride) + field.shape[1:])
    return (shaped, shaped[:, :, 0])


def join_pairs(shaped, new_pairs, field):
    joined = jnp.concatenate([new_pairs[:, :, None], shaped[:, :, 1:]], axis=2)
    return joined.reshape(field.shape)


def forward_core(pair_rows, first, last):
    even_part = pair_rows[:, 0]
    odd_part = pair_rows[:, 1]
    next_even = jnp.concatenate([even_part[1:], even_part[-1:]], axis=0)
    next_even = jnp.where(last, even_part, next_even)
    detail = odd_part - 0.5 * (even_part + next_even)
    prev_detail = jnp.concatenate([detail[:1], detail[:-1]], axis=0)
    prev_detail = jnp.where(first, detail, prev_detail)
    smooth = even_part + 0.25 * (prev_detail + detail)
    return jnp.stack([smooth, detail], axis=1)


def inverse_core(pair_rows, first, last):
    smooth = pair_rows[:, 0]
    detail = pair_rows[:, 1]
    prev_detail = jnp.concatenate([detail[:1], detail[:-1]], axis=0)
    prev_detail = jnp.where(first, detail, prev_detail)
    even_part = smooth - 0.25 * (prev_detail + detail)
    next_even = jnp.concatenate([even_part[1:], even_part[-1:]], axis=0)
    next_even = jnp.where(last, even_part, next_even)
    odd_part = detail + 0.5 * (even_part + next_even)
    return jnp.stack([even_part, odd_part], axis=1)


def level(field, stride, enabled, forward, width, length, is_first, is_last):
    shaped, pair_rows = split_pairs(field, stride)
    pair_ids = jnp.arange(pair_rows.shape[0], dtype=jnp.int32).reshape(
        (-1,) + (1,) * (pair_rows.ndim - 2)
    )
    first = is_first & (pair_ids == width // (2 * stride))
    last = is_last & (pair_ids == (width + length) // (2 * stride) - 1)
    core = forward_core if forward else inverse_core
    new_pairs = core(pair_rows, first, last)
    return jnp.where(enabled, join_pairs(shaped, new_pairs, field), field)


PAD = 8


def _lift_level(work, stride, enabled, forward, width, length, ends, axis=0):
    rows = work.shape[axis] - 2 * PAD
    pairs = rows // (2 * stride)
    step = 2 * stride
    shape = list(work.shape)
    shape[axis] = pairs
    pair_ids = lax.broadcasted_iota(jnp.int32, tuple(shape), axis)
    first = (pair_ids == width // step) & (ends[0] != 0)
    last = (pair_ids == (width + length) // step - 1) & (ends[1] != 0)

    def at(start):
        window = pl.ds(start, pairs, stride=step)
        return (window,) if axis == 0 else (slice(None), window)

    evens = at(PAD)
    odds = at(PAD + stride)
    next_evens = at(PAD + step)
    prev_odds = at(PAD - stride)
    if forward:
        even_part = work[evens]
        odd_part = work[odds]
        next_even = jnp.where(last, even_part, work[next_evens])
        detail = odd_part - 0.5 * (even_part + next_even)
        work[odds] = jnp.where(enabled, detail, odd_part)
        prev_detail = jnp.where(first, detail, work[prev_odds])
        smooth = even_part + 0.25 * (prev_detail + detail)
        work[evens] = jnp.where(enabled, smooth, even_part)
    else:
        smooth = work[evens]
        detail = work[odds]
        prev_detail = jnp.where(first, detail, work[prev_odds])
        even_part = smooth - 0.25 * (prev_detail + detail)
        work[evens] = jnp.where(enabled, even_part, smooth)
        next_even = jnp.where(last, even_part, work[next_evens])
        odd_part = detail + 0.5 * (even_part + next_even)
        work[odds] = jnp.where(enabled, odd_part, detail)


def _rcv_kernel(ends_ref, depth_ref, thr_ref, left_ref, mid_ref, right_ref, out_ref, work, *, width):
    length = mid_ref.shape[1]
    ends = (ends_ref[0], ends_ref[1])
    depth = depth_ref[...]
    work[:, PAD : PAD + width] = left_ref[...]
    work[:, PAD + width : PAD + width + length] = mid_ref[...]
    work[:, PAD + width + length : PAD + 2 * width + length] = right_ref[...]
    for depth_index in range(LEVELS):
        _lift_level(work, 2**depth_index, depth > depth_index, True, width, length, ends, axis=1)
    field = work[:, PAD : PAD + 2 * width + length]
    thr = thr_ref[...]
    work[:, PAD : PAD + 2 * width + length] = field - jnp.clip(field, -thr, thr)
    for depth_index in reversed(range(LEVELS)):
        _lift_level(work, 2**depth_index, depth > depth_index, False, width, length, ends, axis=1)
    out_ref[...] = work[:, PAD + width : PAD + width + length]


def rcv_stage(left, mid, right, thr, ends, depth, width):
    rows, cols, samples = mid.shape
    smem = pl.BlockSpec(memory_space=pltpu.SMEM)
    vmem = pl.BlockSpec(memory_space=pltpu.VMEM)
    return pl.pallas_call(
        functools.partial(_rcv_kernel, width=width),
        out_shape=jax.ShapeDtypeStruct(mid.shape, jnp.float32),
        in_specs=[smem] + [vmem] * 5,
        out_specs=vmem,
        scratch_shapes=[pltpu.VMEM((rows, cols + 2 * width + 2 * PAD, samples), jnp.float32)],
    )(ends, depth, thr, left, mid, right)


def _stage_kernel(*refs, kind, width, length, out_from, out_rows):
    if kind == "fwd":
        ends_ref, depth_ref, terms_ref, out_ref, work = refs
    elif kind == "both":
        ends_ref, depth_ref, thr_ref, in_ref, out_ref, work = refs
    else:
        ends_ref, depth_ref, in_ref, out_ref, work = refs
    rows = work.shape[0] - 2 * PAD
    ends = (ends_ref[0], ends_ref[1])
    depth = depth_ref[...]
    if kind == "fwd":
        work[PAD : PAD + rows] = 0.5 * (
            terms_ref[:, 0].astype(jnp.float32) + terms_ref[:, 1].astype(jnp.float32)
        )
    else:
        work[PAD : PAD + rows] = in_ref[...]
    if kind != "inv":
        for depth_index in range(LEVELS):
            _lift_level(work, 2**depth_index, depth > depth_index, True, width, length, ends)
    if kind == "both":
        field = work[PAD : PAD + rows]
        thr = thr_ref[...]
        work[PAD : PAD + rows] = field - jnp.clip(field, -thr, thr)
    if kind != "fwd":
        for depth_index in reversed(range(LEVELS)):
            _lift_level(work, 2**depth_index, depth > depth_index, False, width, length, ends)
    out_ref[...] = work[PAD + out_from : PAD + out_from + out_rows]


def lift_stage(kind, operands, ends, depth, width, length, out_from, out_rows):
    rows = operands[-1].shape[0]
    cols, samples = operands[-1].shape[-2:]
    kernel = functools.partial(
        _stage_kernel, kind=kind, width=width, length=length, out_from=out_from, out_rows=out_rows
    )
    smem = pl.BlockSpec(memory_space=pltpu.SMEM)
    vmem = pl.BlockSpec(memory_space=pltpu.VMEM)
    return pl.pallas_call(
        kernel,
        out_shape=jax.ShapeDtypeStruct((out_rows, cols, samples), jnp.float32),
        in_specs=[smem] + [vmem] * (1 + len(operands)),
        out_specs=vmem,
        scratch_shapes=[pltpu.VMEM((rows + 2 * PAD, cols, samples), jnp.float32)],
    )(ends, depth, *operands)


def halos(cells, axis_name, dim, width):
    count = lax.axis_size(axis_name)
    length = cells.shape[dim]
    head = lax.slice_in_dim(cells, 0, width, axis=dim)
    tail = lax.slice_in_dim(cells, length - width, length, axis=dim)
    from_left = lax.ppermute(tail, axis_name, [(i, i + 1) for i in range(count - 1)])
    from_right = lax.ppermute(head, axis_name, [(i + 1, i) for i in range(count - 1)])
    return from_left, from_right


def extend(cells, axis_name, dim, width):
    from_left, from_right = halos(cells, axis_name, dim, width)
    return jnp.concatenate([from_left, cells, from_right], axis=dim)


def body(observed, estimate, acquired, levels, thresholds):
    src_count = lax.axis_size("src")
    rcv_count = lax.axis_size("rcv")
    src_index = lax.axis_index("src")
    rcv_index = lax.axis_index("rcv")
    row_count, col_count, samples = observed.shape
    extent = row_count * src_count
    blocks = acquired.shape[0]
    block_size = extent // blocks
    block_ids = jnp.arange(blocks, dtype=jnp.int32)
    row_ids = src_index * row_count + jnp.arange(row_count, dtype=jnp.int32)
    col_ids = rcv_index * col_count + jnp.arange(col_count, dtype=jnp.int32)
    pick_rows = (row_ids[:, None] // block_size == block_ids[None, :]).astype(jnp.float32)
    pick_cols = (col_ids[:, None] // block_size == block_ids[None, :]).astype(jnp.float32)
    row_mask = jnp.dot(pick_rows, acquired.astype(jnp.float32), precision=lax.Precision.HIGHEST)
    local_mask = jnp.dot(row_mask, pick_cols.T, precision=lax.Precision.HIGHEST)
    est_float = estimate.astype(jnp.float32)
    merged = (
        est_float + local_mask[:, :, None] * (observed.astype(jnp.float32) - est_float)
    ).astype(jnp.bfloat16)

    assert rcv_count == 2 * src_count and row_count == 2 * col_count
    pieces = merged.reshape(2, col_count, col_count, samples)
    own_part = rcv_index % 2
    perm = [
        (a * rcv_count + b, (b // 2) * rcv_count + 2 * a + b % 2)
        for a in range(src_count)
        for b in range(rcv_count)
    ]
    block = lax.ppermute(pieces, ("src", "rcv"), perm)
    keep = jnp.where(own_part == 0, block[0], block[1])
    give = jnp.where(own_part == 0, block[1], block[0])
    got = lax.ppermute(give, "rcv", [(b, b ^ 1) for b in range(rcv_count)])
    first = jnp.where(own_part == 0, keep, got)
    second = jnp.where(own_part == 0, got, keep)
    mirror = jnp.concatenate(
        [jnp.transpose(first, (1, 0, 2)), jnp.transpose(second, (1, 0, 2))], axis=0
    )
    mirror_halo = 2 * SRC_HALO
    terms = extend(jnp.stack([merged, mirror], axis=1), "src", 0, mirror_halo)

    samples_shape = (1, 1, samples)
    src_depth = levels[0].reshape(samples_shape)
    rcv_depth = levels[1].reshape(samples_shape)
    src_ends = jnp.stack([src_index == 0, src_index == src_count - 1]).astype(jnp.int32)
    rcv_ends = jnp.stack([rcv_index == 0, rcv_index == rcv_count - 1]).astype(jnp.int32)

    coeff = lift_stage(
        "fwd", (terms,), src_ends, src_depth, mirror_halo, row_count,
        mirror_halo - SRC_HALO, row_count + 2 * SRC_HALO,
    )

    from_left, from_right = halos(coeff, "rcv", 1, RCV_HALO)
    coeff = rcv_stage(
        from_left, coeff, from_right, thresholds.reshape(samples_shape), rcv_ends, rcv_depth, RCV_HALO
    )
    return lift_stage("inv", (coeff,), src_ends, src_depth, SRC_HALO, row_count, SRC_HALO, row_count)

def solution(mesh):
    return jax.shard_map(
        body,
        mesh=mesh,
        in_specs=(P("src", "rcv", None), P("src", "rcv", None), P(), P(), P()),
        out_specs=P("src", "rcv", None),
        check_vma=False,
    )
```

```python
import functools

import jax
import jax.numpy as jnp
from jax import lax
from jax.sharding import PartitionSpec as P
from jax.experimental import pallas as pl
from jax.experimental.pallas import tpu as pltpu

LEVELS = 3
FAR_LEFT, FAR_RIGHT = 14, 15
NEAR_LEFT, NEAR_RIGHT = 4, 5
SLOT, NEAR_SLOT = 16, 8


PAD = 8


def _lift_level(work, stride, enabled, forward, width, length, ends, axis=0):
    rows = work.shape[axis] - 2 * PAD
    pairs = rows // (2 * stride)
    step = 2 * stride
    shape = list(work.shape)
    shape[axis] = pairs
    pair_ids = lax.broadcasted_iota(jnp.int32, tuple(shape), axis)
    first = (pair_ids == width // step) & (ends[0] != 0)
    last = (pair_ids == (width + length) // step - 1) & (ends[1] != 0)

    def at(start):
        window = pl.ds(start, pairs, stride=step)
        return (window,) if axis == 0 else (slice(None), window)

    evens = at(PAD)
    odds = at(PAD + stride)
    next_evens = at(PAD + step)
    prev_odds = at(PAD - stride)
    if forward:
        even_part = work[evens]
        odd_part = work[odds]
        next_even = jnp.where(last, even_part, work[next_evens])
        detail = odd_part - 0.5 * (even_part + next_even)
        work[odds] = jnp.where(enabled, detail, odd_part)
        prev_detail = jnp.where(first, detail, work[prev_odds])
        smooth = even_part + 0.25 * (prev_detail + detail)
        work[evens] = jnp.where(enabled, smooth, even_part)
    else:
        smooth = work[evens]
        detail = work[odds]
        prev_detail = jnp.where(first, detail, work[prev_odds])
        even_part = smooth - 0.25 * (prev_detail + detail)
        work[evens] = jnp.where(enabled, even_part, smooth)
        next_even = jnp.where(last, even_part, work[next_evens])
        odd_part = detail + 0.5 * (even_part + next_even)
        work[odds] = jnp.where(enabled, odd_part, detail)


def _fill(work, axis, parts, total):
    def span(lo, hi):
        return (slice(lo, hi),) if axis == 0 else (slice(None), slice(lo, hi))

    cursor = 0
    for offset, value in parts:
        if offset > cursor:
            shape = list(work.shape)
            shape[axis] = offset - cursor
            work[span(cursor, offset)] = jnp.zeros(shape, work.dtype)
        size = value.shape[axis]
        work[span(offset, offset + size)] = value
        cursor = offset + size
    if total > cursor:
        shape = list(work.shape)
        shape[axis] = total - cursor
        work[span(cursor, total)] = jnp.zeros(shape, work.dtype)


def _src_forward_kernel(
    ends_ref, depth_ref, left_ref, merged_ref, mirror_ref, right_ref, out_ref, work, *, width, out_from
):
    length = merged_ref.shape[0]
    ends = (ends_ref[0], ends_ref[1])
    depth = depth_ref[...]

    def half_sum(ref):
        return 0.5 * (ref[:, 0].astype(jnp.float32) + ref[:, 1].astype(jnp.float32))

    body = 0.5 * (merged_ref[...].astype(jnp.float32) + mirror_ref[...].astype(jnp.float32))
    parts = [
        (PAD + width - left_ref.shape[0], half_sum(left_ref)),
        (PAD + width, body),
        (PAD + width + length, half_sum(right_ref)),
    ]
    _fill(work, 0, parts, work.shape[0])
    for depth_index in range(LEVELS):
        _lift_level(work, 2**depth_index, depth > depth_index, True, width, length, ends)
    out_ref[...] = work[PAD + width - out_from : PAD + width - out_from + out_ref.shape[0]]


def _src_inverse_kernel(ends_ref, depth_ref, in_ref, out_ref, work, *, width, in_from):
    length = out_ref.shape[0]
    ends = (ends_ref[0], ends_ref[1])
    depth = depth_ref[...]
    _fill(work, 0, [(PAD + width - in_from, in_ref[...])], work.shape[0])
    for depth_index in reversed(range(LEVELS)):
        _lift_level(work, 2**depth_index, depth > depth_index, False, width, length, ends)
    out_ref[...] = work[PAD + width : PAD + width + length]


def _rcv_kernel(ends_ref, depth_ref, thr_ref, left_ref, mid_ref, right_ref, out_ref, work, *, width):
    length = mid_ref.shape[1]
    ends = (ends_ref[0], ends_ref[1])
    depth = depth_ref[...]
    parts = [
        (PAD + width - left_ref.shape[1], left_ref[...]),
        (PAD + width, mid_ref[...]),
        (PAD + width + length, right_ref[...]),
    ]
    _fill(work, 1, parts, work.shape[1])
    for depth_index in range(LEVELS):
        _lift_level(work, 2**depth_index, depth > depth_index, True, width, length, ends, axis=1)
    field = work[:, PAD : PAD + 2 * width + length]
    thr = thr_ref[...]
    work[:, PAD : PAD + 2 * width + length] = field - jnp.clip(field, -thr, thr)
    for depth_index in reversed(range(LEVELS)):
        _lift_level(work, 2**depth_index, depth > depth_index, False, width, length, ends, axis=1)
    out_ref[...] = work[:, PAD + width : PAD + width + length]


def _call(kernel, out_shape, scratch_shape, *operands):
    smem = pl.BlockSpec(memory_space=pltpu.SMEM)
    vmem = pl.BlockSpec(memory_space=pltpu.VMEM)
    return pl.pallas_call(
        kernel,
        out_shape=jax.ShapeDtypeStruct(out_shape, jnp.float32),
        in_specs=[smem] + [vmem] * (len(operands) - 1),
        out_specs=vmem,
        scratch_shapes=[pltpu.VMEM(scratch_shape, jnp.float32)],
    )(*operands)


def halos(cells, axis_name, dim, left_width, right_width):
    count = lax.axis_size(axis_name)
    length = cells.shape[dim]
    head = lax.slice_in_dim(cells, 0, right_width, axis=dim)
    tail = lax.slice_in_dim(cells, length - left_width, length, axis=dim)
    from_left = lax.ppermute(tail, axis_name, [(i, i + 1) for i in range(count - 1)])
    from_right = lax.ppermute(head, axis_name, [(i + 1, i) for i in range(count - 1)])
    return from_left, from_right


def body(observed, estimate, acquired, levels, thresholds):
    src_count = lax.axis_size("src")
    rcv_count = lax.axis_size("rcv")
    src_index = lax.axis_index("src")
    rcv_index = lax.axis_index("rcv")
    row_count, col_count, samples = observed.shape
    extent = row_count * src_count
    blocks = acquired.shape[0]
    block_size = extent // blocks
    block_ids = jnp.arange(blocks, dtype=jnp.int32)
    row_ids = src_index * row_count + jnp.arange(row_count, dtype=jnp.int32)
    col_ids = rcv_index * col_count + jnp.arange(col_count, dtype=jnp.int32)
    pick_rows = (row_ids[:, None] // block_size == block_ids[None, :]).astype(jnp.float32)
    pick_cols = (col_ids[:, None] // block_size == block_ids[None, :]).astype(jnp.float32)
    row_mask = jnp.dot(pick_rows, acquired.astype(jnp.float32), precision=lax.Precision.HIGHEST)
    local_mask = jnp.dot(row_mask, pick_cols.T, precision=lax.Precision.HIGHEST)
    est_float = estimate.astype(jnp.float32)
    merged = (
        est_float + local_mask[:, :, None] * (observed.astype(jnp.float32) - est_float)
    ).astype(jnp.bfloat16)

    ratio = rcv_count // src_count
    pieces = merged.reshape(ratio, col_count, col_count, samples)
    own_part = rcv_index % ratio
    received = []
    for shift in range(ratio):
        perm = []
        for a in range(src_count):
            for b in range(rcv_count):
                part = (b % ratio + shift) % ratio
                perm.append((a * rcv_count + b, (b // ratio) * rcv_count + a * ratio + part))
        send = lax.dynamic_index_in_dim(pieces, (own_part + shift) % ratio, axis=0, keepdims=False)
        received.append(lax.ppermute(send, ("src", "rcv"), perm))
    received = jnp.stack(received)
    slots = []
    for slot in range(ratio):
        got = lax.dynamic_index_in_dim(received, (own_part - slot) % ratio, axis=0, keepdims=False)
        slots.append(jnp.transpose(got, (1, 0, 2)))
    mirror = jnp.concatenate(slots, axis=0)
    samples_shape = (1, 1, samples)
    src_depth = levels[0].reshape(samples_shape)
    rcv_depth = levels[1].reshape(samples_shape)
    src_ends = jnp.stack([src_index == 0, src_index == src_count - 1]).astype(jnp.int32)
    rcv_ends = jnp.stack([rcv_index == 0, rcv_index == rcv_count - 1]).astype(jnp.int32)

    left_src, right_src = halos(jnp.stack([merged, mirror], axis=1), "src", 0, FAR_LEFT, FAR_RIGHT)
    coeff = _call(
        functools.partial(_src_forward_kernel, width=SLOT, out_from=NEAR_LEFT),
        (NEAR_LEFT + row_count + NEAR_RIGHT, col_count, samples),
        (row_count + 2 * SLOT + 2 * PAD, col_count, samples),
        src_ends, src_depth, left_src, merged, mirror, right_src,
    )
    left_rcv, right_rcv = halos(coeff, "rcv", 1, FAR_LEFT, FAR_RIGHT)
    coeff = _call(
        functools.partial(_rcv_kernel, width=SLOT),
        coeff.shape,
        (coeff.shape[0], col_count + 2 * SLOT + 2 * PAD, samples),
        rcv_ends, rcv_depth, thresholds.reshape(samples_shape), left_rcv, coeff, right_rcv,
    )
    return _call(
        functools.partial(_src_inverse_kernel, width=NEAR_SLOT, in_from=NEAR_LEFT),
        (row_count, col_count, samples),
        (row_count + 2 * NEAR_SLOT + 2 * PAD, col_count, samples),
        src_ends, src_depth, coeff,
    )

def solution(mesh):
    return jax.shard_map(
        body,
        mesh=mesh,
        in_specs=(P("src", "rcv", None), P("src", "rcv", None), P(), P(), P()),
        out_specs=P("src", "rcv", None),
        check_vma=False,
    )
```

```python
import functools

import jax
import jax.numpy as jnp
from jax import lax
from jax.sharding import PartitionSpec as P
from jax.experimental import pallas as pl
from jax.experimental.pallas import tpu as pltpu

LEVELS = 3
FAR_LEFT, FAR_RIGHT = 14, 15
NEAR_LEFT, NEAR_RIGHT = 4, 5
SLOT, NEAR_SLOT = 16, 8


PAD = 8


def _lift_level(work, stride, enabled, forward, width, length, ends, axis=0):
    rows = work.shape[axis] - 2 * PAD
    pairs = rows // (2 * stride)
    step = 2 * stride
    shape = list(work.shape)
    shape[axis] = pairs
    pair_ids = lax.broadcasted_iota(jnp.int32, tuple(shape), axis)
    first = (pair_ids == width // step) & (ends[0] != 0)
    last = (pair_ids == (width + length) // step - 1) & (ends[1] != 0)

    def at(start):
        window = pl.ds(start, pairs, stride=step)
        return (window,) if axis == 0 else (slice(None), window)

    evens = at(PAD)
    odds = at(PAD + stride)
    next_evens = at(PAD + step)
    prev_odds = at(PAD - stride)
    if forward:
        even_part = work[evens]
        odd_part = work[odds]
        next_even = jnp.where(last, even_part, work[next_evens])
        detail = odd_part - 0.5 * (even_part + next_even)
        work[odds] = jnp.where(enabled, detail, odd_part)
        prev_detail = jnp.where(first, detail, work[prev_odds])
        smooth = even_part + 0.25 * (prev_detail + detail)
        work[evens] = jnp.where(enabled, smooth, even_part)
    else:
        smooth = work[evens]
        detail = work[odds]
        prev_detail = jnp.where(first, detail, work[prev_odds])
        even_part = smooth - 0.25 * (prev_detail + detail)
        work[evens] = jnp.where(enabled, even_part, smooth)
        next_even = jnp.where(last, even_part, work[next_evens])
        odd_part = detail + 0.5 * (even_part + next_even)
        work[odds] = jnp.where(enabled, odd_part, detail)


def _fill(work, axis, parts, total):
    def span(lo, hi):
        return (slice(lo, hi),) if axis == 0 else (slice(None), slice(lo, hi))

    cursor = 0
    for offset, value in parts:
        if offset > cursor:
            shape = list(work.shape)
            shape[axis] = offset - cursor
            work[span(cursor, offset)] = jnp.zeros(shape, work.dtype)
        size = value.shape[axis]
        work[span(offset, offset + size)] = value
        cursor = offset + size
    if total > cursor:
        shape = list(work.shape)
        shape[axis] = total - cursor
        work[span(cursor, total)] = jnp.zeros(shape, work.dtype)


def _src_forward_kernel(
    ends_ref, depth_ref, left_ref, merged_ref, mirror_ref, right_ref, out_ref, work, *, width, out_from
):
    length = merged_ref.shape[0]
    ends = (ends_ref[0], ends_ref[1])
    depth = depth_ref[...]

    def half_sum(ref):
        return 0.5 * (ref[:, 0].astype(jnp.float32) + ref[:, 1].astype(jnp.float32))

    body = 0.5 * (merged_ref[...].astype(jnp.float32) + mirror_ref[...].astype(jnp.float32))
    parts = [
        (PAD + width - left_ref.shape[0], half_sum(left_ref)),
        (PAD + width, body),
        (PAD + width + length, half_sum(right_ref)),
    ]
    _fill(work, 0, parts, work.shape[0])
    for depth_index in range(LEVELS):
        _lift_level(work, 2**depth_index, depth > depth_index, True, width, length, ends)
    out_ref[...] = work[PAD + width - out_from : PAD + width - out_from + out_ref.shape[0]]


def _rcv_kernel(
    rcv_ends_ref, src_ends_ref, rcv_depth_ref, src_depth_ref, thr_ref, left_ref, mid_ref, right_ref,
    out_ref, work, rows_work, *, width, src_width, in_from,
):
    length = mid_ref.shape[1]
    ends = (rcv_ends_ref[0], rcv_ends_ref[1])
    depth = rcv_depth_ref[...]
    parts = [
        (PAD + width - left_ref.shape[1], left_ref[...]),
        (PAD + width, mid_ref[...]),
        (PAD + width + length, right_ref[...]),
    ]
    _fill(work, 1, parts, work.shape[1])
    for depth_index in range(LEVELS):
        _lift_level(work, 2**depth_index, depth > depth_index, True, width, length, ends, axis=1)
    field = work[:, PAD : PAD + 2 * width + length]
    thr = thr_ref[...]
    work[:, PAD : PAD + 2 * width + length] = field - jnp.clip(field, -thr, thr)
    for depth_index in reversed(range(LEVELS)):
        _lift_level(work, 2**depth_index, depth > depth_index, False, width, length, ends, axis=1)

    row_count = out_ref.shape[0]
    ends = (src_ends_ref[0], src_ends_ref[1])
    depth = src_depth_ref[...]
    block = work[:, PAD + width : PAD + width + length]
    _fill(rows_work, 0, [(PAD + src_width - in_from, block)], rows_work.shape[0])
    for depth_index in reversed(range(LEVELS)):
        _lift_level(rows_work, 2**depth_index, depth > depth_index, False, src_width, row_count, ends)
    out_ref[...] = rows_work[PAD + src_width : PAD + src_width + row_count]


def _call(kernel, out_shape, scratch_shapes, smem_count, *operands):
    smem = pl.BlockSpec(memory_space=pltpu.SMEM)
    vmem = pl.BlockSpec(memory_space=pltpu.VMEM)
    return pl.pallas_call(
        kernel,
        out_shape=jax.ShapeDtypeStruct(out_shape, jnp.float32),
        in_specs=[smem] * smem_count + [vmem] * (len(operands) - smem_count),
        out_specs=vmem,
        scratch_shapes=[pltpu.VMEM(shape, jnp.float32) for shape in scratch_shapes],
    )(*operands)


def halos(cells, axis_name, dim, left_width, right_width):
    count = lax.axis_size(axis_name)
    length = cells.shape[dim]
    head = lax.slice_in_dim(cells, 0, right_width, axis=dim)
    tail = lax.slice_in_dim(cells, length - left_width, length, axis=dim)
    from_left = lax.ppermute(tail, axis_name, [(i, i + 1) for i in range(count - 1)])
    from_right = lax.ppermute(head, axis_name, [(i + 1, i) for i in range(count - 1)])
    return from_left, from_right


def body(observed, estimate, acquired, levels, thresholds):
    src_count = lax.axis_size("src")
    rcv_count = lax.axis_size("rcv")
    src_index = lax.axis_index("src")
    rcv_index = lax.axis_index("rcv")
    row_count, col_count, samples = observed.shape
    extent = row_count * src_count
    blocks = acquired.shape[0]
    block_size = extent // blocks
    block_ids = jnp.arange(blocks, dtype=jnp.int32)
    row_ids = src_index * row_count + jnp.arange(row_count, dtype=jnp.int32)
    col_ids = rcv_index * col_count + jnp.arange(col_count, dtype=jnp.int32)
    pick_rows = (row_ids[:, None] // block_size == block_ids[None, :]).astype(jnp.float32)
    pick_cols = (col_ids[:, None] // block_size == block_ids[None, :]).astype(jnp.float32)
    row_mask = jnp.dot(pick_rows, acquired.astype(jnp.float32), precision=lax.Precision.HIGHEST)
    local_mask = jnp.dot(row_mask, pick_cols.T, precision=lax.Precision.HIGHEST)
    est_float = estimate.astype(jnp.float32)
    merged = (
        est_float + local_mask[:, :, None] * (observed.astype(jnp.float32) - est_float)
    ).astype(jnp.bfloat16)

    ratio = rcv_count // src_count
    pieces = merged.reshape(ratio, col_count, col_count, samples)
    own_part = rcv_index % ratio
    received = []
    for shift in range(ratio):
        perm = []
        for a in range(src_count):
            for b in range(rcv_count):
                part = (b % ratio + shift) % ratio
                perm.append((a * rcv_count + b, (b // ratio) * rcv_count + a * ratio + part))
        send = lax.dynamic_index_in_dim(pieces, (own_part + shift) % ratio, axis=0, keepdims=False)
        received.append(lax.ppermute(send, ("src", "rcv"), perm))
    received = jnp.stack(received)
    slots = []
    for slot in range(ratio):
        got = lax.dynamic_index_in_dim(received, (own_part - slot) % ratio, axis=0, keepdims=False)
        slots.append(jnp.transpose(got, (1, 0, 2)))
    mirror = jnp.concatenate(slots, axis=0)
    samples_shape = (1, 1, samples)
    src_depth = levels[0].reshape(samples_shape)
    rcv_depth = levels[1].reshape(samples_shape)
    src_ends = jnp.stack([src_index == 0, src_index == src_count - 1]).astype(jnp.int32)
    rcv_ends = jnp.stack([rcv_index == 0, rcv_index == rcv_count - 1]).astype(jnp.int32)

    left_src, right_src = halos(jnp.stack([merged, mirror], axis=1), "src", 0, FAR_LEFT, FAR_RIGHT)
    coeff = _call(
        functools.partial(_src_forward_kernel, width=SLOT, out_from=NEAR_LEFT),
        (NEAR_LEFT + row_count + NEAR_RIGHT, col_count, samples),
        [(row_count + 2 * SLOT + 2 * PAD, col_count, samples)],
        1,
        src_ends, src_depth, left_src, merged, mirror, right_src,
    )
    left_rcv, right_rcv = halos(coeff, "rcv", 1, FAR_LEFT, FAR_RIGHT)
    return _call(
        functools.partial(_rcv_kernel, width=SLOT, src_width=NEAR_SLOT, in_from=NEAR_LEFT),
        (row_count, col_count, samples),
        [
            (coeff.shape[0], col_count + 2 * SLOT + 2 * PAD, samples),
            (row_count + 2 * NEAR_SLOT + 2 * PAD, col_count, samples),
        ],
        2,
        rcv_ends, src_ends, rcv_depth, src_depth, thresholds.reshape(samples_shape),
        left_rcv, coeff, right_rcv,
    )

def solution(mesh):
    return jax.shard_map(
        body,
        mesh=mesh,
        in_specs=(P("src", "rcv", None), P("src", "rcv", None), P(), P(), P()),
        out_specs=P("src", "rcv", None),
        check_vma=False,
    )
```

```python
import functools

import jax
import jax.numpy as jnp
from jax import lax
from jax.sharding import PartitionSpec as P
from jax.experimental import pallas as pl
from jax.experimental.pallas import tpu as pltpu

LEVELS = 3
FAR_LEFT, FAR_RIGHT = 14, 15
NEAR_LEFT, NEAR_RIGHT = 4, 5
SLOT, NEAR_SLOT = 16, 8


PAD = 8


def _lift_level(work, stride, enabled, forward, width, length, ends, axis=0):
    rows = work.shape[axis] - 2 * PAD
    pairs = rows // (2 * stride)
    step = 2 * stride
    shape = list(work.shape)
    shape[axis] = pairs
    pair_ids = lax.broadcasted_iota(jnp.int32, tuple(shape), axis)
    first = (pair_ids == width // step) & (ends[0] != 0)
    last = (pair_ids == (width + length) // step - 1) & (ends[1] != 0)

    def at(start):
        window = pl.ds(start, pairs, stride=step)
        return (window,) if axis == 0 else (slice(None), window)

    evens = at(PAD)
    odds = at(PAD + stride)
    next_evens = at(PAD + step)
    prev_odds = at(PAD - stride)
    if forward:
        even_part = work[evens]
        odd_part = work[odds]
        next_even = jnp.where(last, even_part, work[next_evens])
        detail = odd_part - 0.5 * (even_part + next_even)
        work[odds] = jnp.where(enabled, detail, odd_part)
        prev_detail = jnp.where(first, detail, work[prev_odds])
        smooth = even_part + 0.25 * (prev_detail + detail)
        work[evens] = jnp.where(enabled, smooth, even_part)
    else:
        smooth = work[evens]
        detail = work[odds]
        prev_detail = jnp.where(first, detail, work[prev_odds])
        even_part = smooth - 0.25 * (prev_detail + detail)
        work[evens] = jnp.where(enabled, even_part, smooth)
        next_even = jnp.where(last, even_part, work[next_evens])
        odd_part = detail + 0.5 * (even_part + next_even)
        work[odds] = jnp.where(enabled, odd_part, detail)


def _fill(work, axis, parts, total):
    def span(lo, hi):
        return (slice(lo, hi),) if axis == 0 else (slice(None), slice(lo, hi))

    cursor = 0
    for offset, value in parts:
        if offset > cursor:
            shape = list(work.shape)
            shape[axis] = offset - cursor
            work[span(cursor, offset)] = jnp.zeros(shape, work.dtype)
        size = value.shape[axis]
        work[span(offset, offset + size)] = value
        cursor = offset + size
    if total > cursor:
        shape = list(work.shape)
        shape[axis] = total - cursor
        work[span(cursor, total)] = jnp.zeros(shape, work.dtype)


def _src_forward_kernel(
    ends_ref, depth_ref, left_ref, merged_ref, mirror_ref, right_ref, out_ref, work, *, width, out_from
):
    length = merged_ref.shape[0]
    ends = (ends_ref[0], ends_ref[1])
    depth = depth_ref[...]

    def half_sum(ref):
        return 0.5 * (ref[:, 0].astype(jnp.float32) + ref[:, 1].astype(jnp.float32))

    body = 0.5 * (merged_ref[...].astype(jnp.float32) + mirror_ref[...].astype(jnp.float32))
    parts = [
        (PAD + width - left_ref.shape[0], half_sum(left_ref)),
        (PAD + width, body),
        (PAD + width + length, half_sum(right_ref)),
    ]
    _fill(work, 0, parts, work.shape[0])
    for depth_index in range(LEVELS):
        _lift_level(work, 2**depth_index, depth > depth_index, True, width, length, ends)
    out_ref[...] = work[PAD + width - out_from : PAD + width - out_from + out_ref.shape[0]]


def _rcv_kernel(
    rcv_ends_ref, src_ends_ref, rcv_depth_ref, src_depth_ref, thr_ref, left_ref, mid_ref, right_ref,
    out_ref, work, rows_work, *, width, src_width, in_from,
):
    length = mid_ref.shape[1]
    ends = (rcv_ends_ref[0], rcv_ends_ref[1])
    depth = rcv_depth_ref[...]
    parts = [
        (PAD + width - left_ref.shape[1], left_ref[...]),
        (PAD + width, mid_ref[...]),
        (PAD + width + length, right_ref[...]),
    ]
    _fill(work, 1, parts, work.shape[1])
    for depth_index in range(LEVELS):
        _lift_level(work, 2**depth_index, depth > depth_index, True, width, length, ends, axis=1)
    field = work[:, PAD : PAD + 2 * width + length]
    thr = thr_ref[...]
    work[:, PAD : PAD + 2 * width + length] = field - jnp.clip(field, -thr, thr)
    for depth_index in reversed(range(LEVELS)):
        _lift_level(work, 2**depth_index, depth > depth_index, False, width, length, ends, axis=1)

    row_count = out_ref.shape[0]
    ends = (src_ends_ref[0], src_ends_ref[1])
    depth = src_depth_ref[...]
    block = work[:, PAD + width : PAD + width + length]
    _fill(rows_work, 0, [(PAD + src_width - in_from, block)], rows_work.shape[0])
    for depth_index in reversed(range(LEVELS)):
        _lift_level(rows_work, 2**depth_index, depth > depth_index, False, src_width, row_count, ends)
    out_ref[...] = rows_work[PAD + src_width : PAD + src_width + row_count]


def _call(kernel, out_shape, scratch_shapes, smem_count, *operands):
    smem = pl.BlockSpec(memory_space=pltpu.SMEM)
    vmem = pl.BlockSpec(memory_space=pltpu.VMEM)
    return pl.pallas_call(
        kernel,
        out_shape=jax.ShapeDtypeStruct(out_shape, jnp.float32),
        in_specs=[smem] * smem_count + [vmem] * (len(operands) - smem_count),
        out_specs=vmem,
        scratch_shapes=[pltpu.VMEM(shape, jnp.float32) for shape in scratch_shapes],
    )(*operands)


def halos(cells, axis_name, dim, left_width, right_width):
    count = lax.axis_size(axis_name)
    length = cells.shape[dim]
    head = lax.slice_in_dim(cells, 0, right_width, axis=dim)
    tail = lax.slice_in_dim(cells, length - left_width, length, axis=dim)
    from_left = lax.ppermute(tail, axis_name, [(i, i + 1) for i in range(count - 1)])
    from_right = lax.ppermute(head, axis_name, [(i + 1, i) for i in range(count - 1)])
    return from_left, from_right


def body(observed, estimate, acquired, levels, thresholds):
    src_count = lax.axis_size("src")
    rcv_count = lax.axis_size("rcv")
    src_index = lax.axis_index("src")
    rcv_index = lax.axis_index("rcv")
    row_count, col_count, samples = observed.shape
    extent = row_count * src_count
    blocks = acquired.shape[0]
    block_size = extent // blocks
    if block_size % row_count == 0 and block_size % col_count == 0:
        local_mask = acquired[
            src_index * row_count // block_size, rcv_index * col_count // block_size
        ].astype(jnp.float32)
    else:
        block_ids = jnp.arange(blocks, dtype=jnp.int32)
        row_ids = src_index * row_count + jnp.arange(row_count, dtype=jnp.int32)
        col_ids = rcv_index * col_count + jnp.arange(col_count, dtype=jnp.int32)
        pick_rows = (row_ids[:, None] // block_size == block_ids[None, :]).astype(jnp.float32)
        pick_cols = (col_ids[:, None] // block_size == block_ids[None, :]).astype(jnp.float32)
        row_mask = jnp.dot(pick_rows, acquired.astype(jnp.float32), precision=lax.Precision.HIGHEST)
        local_mask = jnp.dot(row_mask, pick_cols.T, precision=lax.Precision.HIGHEST)[:, :, None]
    est_float = estimate.astype(jnp.float32)
    merged = (
        est_float + local_mask * (observed.astype(jnp.float32) - est_float)
    ).astype(jnp.bfloat16)

    ratio = rcv_count // src_count
    pieces = merged.reshape(ratio, col_count, col_count, samples)
    own_part = rcv_index % ratio
    received = []
    for shift in range(ratio):
        perm = []
        for a in range(src_count):
            for b in range(rcv_count):
                part = (b % ratio + shift) % ratio
                perm.append((a * rcv_count + b, (b // ratio) * rcv_count + a * ratio + part))
        send = lax.dynamic_index_in_dim(pieces, (own_part + shift) % ratio, axis=0, keepdims=False)
        received.append(lax.ppermute(send, ("src", "rcv"), perm))
    received = jnp.stack(received)
    slots = []
    for slot in range(ratio):
        got = lax.dynamic_index_in_dim(received, (own_part - slot) % ratio, axis=0, keepdims=False)
        slots.append(jnp.transpose(got, (1, 0, 2)))
    mirror = jnp.concatenate(slots, axis=0)
    samples_shape = (1, 1, samples)
    src_depth = levels[0].reshape(samples_shape)
    rcv_depth = levels[1].reshape(samples_shape)
    src_ends = jnp.stack([src_index == 0, src_index == src_count - 1]).astype(jnp.int32)
    rcv_ends = jnp.stack([rcv_index == 0, rcv_index == rcv_count - 1]).astype(jnp.int32)

    left_src, right_src = halos(jnp.stack([merged, mirror], axis=1), "src", 0, FAR_LEFT, FAR_RIGHT)
    coeff = _call(
        functools.partial(_src_forward_kernel, width=SLOT, out_from=NEAR_LEFT),
        (NEAR_LEFT + row_count + NEAR_RIGHT, col_count, samples),
        [(row_count + 2 * SLOT + 2 * PAD, col_count, samples)],
        1,
        src_ends, src_depth, left_src, merged, mirror, right_src,
    )
    left_rcv, right_rcv = halos(coeff, "rcv", 1, FAR_LEFT, FAR_RIGHT)
    return _call(
        functools.partial(_rcv_kernel, width=SLOT, src_width=NEAR_SLOT, in_from=NEAR_LEFT),
        (row_count, col_count, samples),
        [
            (coeff.shape[0], col_count + 2 * SLOT + 2 * PAD, samples),
            (row_count + 2 * NEAR_SLOT + 2 * PAD, col_count, samples),
        ],
        2,
        rcv_ends, src_ends, rcv_depth, src_depth, thresholds.reshape(samples_shape),
        left_rcv, coeff, right_rcv,
    )

def solution(mesh):
    return jax.shard_map(
        body,
        mesh=mesh,
        in_specs=(P("src", "rcv", None), P("src", "rcv", None), P(), P(), P()),
        out_specs=P("src", "rcv", None),
        check_vma=False,
    )
```

```python
import functools

import jax
import jax.numpy as jnp
from jax import lax
from jax.sharding import PartitionSpec as P
from jax.experimental import pallas as pl
from jax.experimental.pallas import tpu as pltpu

LEVELS = 3
FAR_LEFT, FAR_RIGHT = 14, 15
NEAR_LEFT, NEAR_RIGHT = 4, 5
SLOT, NEAR_SLOT = 16, 8


PAD = 8


def _lift_level(work, stride, enabled, forward, width, length, ends, axis=0):
    rows = work.shape[axis] - 2 * PAD
    pairs = rows // (2 * stride)
    step = 2 * stride
    shape = list(work.shape)
    shape[axis] = pairs
    pair_ids = lax.broadcasted_iota(jnp.int32, tuple(shape), axis)
    first = (pair_ids == width // step) & (ends[0] != 0)
    last = (pair_ids == (width + length) // step - 1) & (ends[1] != 0)

    def at(start):
        window = pl.ds(start, pairs, stride=step)
        return (window,) if axis == 0 else (slice(None), window)

    evens = at(PAD)
    odds = at(PAD + stride)
    next_evens = at(PAD + step)
    prev_odds = at(PAD - stride)
    if forward:
        even_part = work[evens]
        odd_part = work[odds]
        next_even = jnp.where(last, even_part, work[next_evens])
        detail = odd_part - 0.5 * (even_part + next_even)
        work[odds] = jnp.where(enabled, detail, odd_part)
        prev_detail = jnp.where(first, detail, work[prev_odds])
        smooth = even_part + 0.25 * (prev_detail + detail)
        work[evens] = jnp.where(enabled, smooth, even_part)
    else:
        smooth = work[evens]
        detail = work[odds]
        prev_detail = jnp.where(first, detail, work[prev_odds])
        even_part = smooth - 0.25 * (prev_detail + detail)
        work[evens] = jnp.where(enabled, even_part, smooth)
        next_even = jnp.where(last, even_part, work[next_evens])
        odd_part = detail + 0.5 * (even_part + next_even)
        work[odds] = jnp.where(enabled, odd_part, detail)


def _fill(work, axis, parts, total):
    def span(lo, hi):
        return (slice(lo, hi),) if axis == 0 else (slice(None), slice(lo, hi))

    cursor = 0
    for offset, value in parts:
        if offset > cursor:
            shape = list(work.shape)
            shape[axis] = offset - cursor
            work[span(cursor, offset)] = jnp.zeros(shape, work.dtype)
        size = value.shape[axis]
        work[span(offset, offset + size)] = value
        cursor = offset + size
    if total > cursor:
        shape = list(work.shape)
        shape[axis] = total - cursor
        work[span(cursor, total)] = jnp.zeros(shape, work.dtype)


def _src_forward_kernel(
    ends_ref, depth_ref, left_ref, merged_ref, right_ref, mirror_ref, out_ref, work, *, width, out_from
):
    length = merged_ref.shape[0]
    ends = (ends_ref[0], ends_ref[1])
    depth = depth_ref[...]
    near = left_ref.shape[0]
    far = right_ref.shape[0]

    def term_sum(ref, lo, size):
        return 0.5 * (ref[...].astype(jnp.float32) + mirror_ref[lo : lo + size].astype(jnp.float32))

    parts = [
        (PAD + width - near, term_sum(left_ref, 0, near)),
        (PAD + width, term_sum(merged_ref, near, length)),
        (PAD + width + length, term_sum(right_ref, near + length, far)),
    ]
    _fill(work, 0, parts, work.shape[0])
    for depth_index in range(LEVELS):
        _lift_level(work, 2**depth_index, depth > depth_index, True, width, length, ends)
    out_ref[...] = work[PAD + width - out_from : PAD + width - out_from + out_ref.shape[0]]


def _rcv_kernel(
    rcv_ends_ref, src_ends_ref, rcv_depth_ref, src_depth_ref, thr_ref, left_ref, mid_ref, right_ref,
    out_ref, work, rows_work, *, width, src_width, in_from,
):
    length = mid_ref.shape[1]
    ends = (rcv_ends_ref[0], rcv_ends_ref[1])
    depth = rcv_depth_ref[...]
    parts = [
        (PAD + width - left_ref.shape[1], left_ref[...]),
        (PAD + width, mid_ref[...]),
        (PAD + width + length, right_ref[...]),
    ]
    _fill(work, 1, parts, work.shape[1])
    for depth_index in range(LEVELS):
        _lift_level(work, 2**depth_index, depth > depth_index, True, width, length, ends, axis=1)
    field = work[:, PAD : PAD + 2 * width + length]
    thr = thr_ref[...]
    work[:, PAD : PAD + 2 * width + length] = field - jnp.clip(field, -thr, thr)
    for depth_index in reversed(range(LEVELS)):
        _lift_level(work, 2**depth_index, depth > depth_index, False, width, length, ends, axis=1)

    row_count = out_ref.shape[0]
    ends = (src_ends_ref[0], src_ends_ref[1])
    depth = src_depth_ref[...]
    block = work[:, PAD + width : PAD + width + length]
    _fill(rows_work, 0, [(PAD + src_width - in_from, block)], rows_work.shape[0])
    for depth_index in reversed(range(LEVELS)):
        _lift_level(rows_work, 2**depth_index, depth > depth_index, False, src_width, row_count, ends)
    out_ref[...] = rows_work[PAD + src_width : PAD + src_width + row_count]


def _call(kernel, out_shape, scratch_shapes, smem_count, *operands):
    smem = pl.BlockSpec(memory_space=pltpu.SMEM)
    vmem = pl.BlockSpec(memory_space=pltpu.VMEM)
    return pl.pallas_call(
        kernel,
        out_shape=jax.ShapeDtypeStruct(out_shape, jnp.float32),
        in_specs=[smem] * smem_count + [vmem] * (len(operands) - smem_count),
        out_specs=vmem,
        scratch_shapes=[pltpu.VMEM(shape, jnp.float32) for shape in scratch_shapes],
    )(*operands)


def halos(cells, axis_name, dim, left_width, right_width):
    count = lax.axis_size(axis_name)
    length = cells.shape[dim]
    head = lax.slice_in_dim(cells, 0, right_width, axis=dim)
    tail = lax.slice_in_dim(cells, length - left_width, length, axis=dim)
    from_left = lax.ppermute(tail, axis_name, [(i, i + 1) for i in range(count - 1)])
    from_right = lax.ppermute(head, axis_name, [(i + 1, i) for i in range(count - 1)])
    return from_left, from_right


def body(observed, estimate, acquired, levels, thresholds):
    src_count = lax.axis_size("src")
    rcv_count = lax.axis_size("rcv")
    src_index = lax.axis_index("src")
    rcv_index = lax.axis_index("rcv")
    row_count, col_count, samples = observed.shape
    extent = row_count * src_count
    blocks = acquired.shape[0]
    block_size = extent // blocks
    block_ids = jnp.arange(blocks, dtype=jnp.int32)
    row_ids = src_index * row_count + jnp.arange(row_count, dtype=jnp.int32)
    col_ids = rcv_index * col_count + jnp.arange(col_count, dtype=jnp.int32)
    pick_rows = (row_ids[:, None] // block_size == block_ids[None, :]).astype(jnp.float32)
    pick_cols = (col_ids[:, None] // block_size == block_ids[None, :]).astype(jnp.float32)
    row_mask = jnp.dot(pick_rows, acquired.astype(jnp.float32), precision=lax.Precision.HIGHEST)
    local_mask = jnp.dot(row_mask, pick_cols.T, precision=lax.Precision.HIGHEST)
    est_float = estimate.astype(jnp.float32)
    merged = (
        est_float + local_mask[:, :, None] * (observed.astype(jnp.float32) - est_float)
    ).astype(jnp.bfloat16)

    assert rcv_count == 2 * src_count and row_count == 2 * col_count
    left_cols, right_cols = halos(merged, "rcv", 1, FAR_LEFT, FAR_RIGHT)
    left_src, right_src = halos(merged, "src", 0, FAR_LEFT, FAR_RIGHT)
    wide_cols = col_count + max(FAR_LEFT, FAR_RIGHT)
    spare = jnp.zeros((row_count, wide_cols - col_count - FAR_LEFT, samples), merged.dtype)
    even_block = jnp.concatenate([left_cols, merged, spare], axis=1)
    odd_block = jnp.concatenate([merged, right_cols], axis=1)
    own_part = rcv_index % 2
    block = jnp.where(own_part == 0, even_block, odd_block).reshape(2, col_count, wide_cols, samples)
    received = []
    for shift in range(2):
        perm = []
        for a in range(src_count):
            for b in range(rcv_count):
                part = (b % 2 + shift) % 2
                perm.append((a * rcv_count + b, (b // 2) * rcv_count + a * 2 + part))
        send = jnp.where((own_part + shift) % 2 == 0, block[0], block[1])
        received.append(lax.ppermute(send, ("src", "rcv"), perm))
    from_even = jnp.where(own_part == 0, received[0], received[1])
    from_odd = jnp.where(own_part == 0, received[1], received[0])
    mirror = jnp.concatenate(
        [
            jnp.transpose(from_even[:, : FAR_LEFT + col_count], (1, 0, 2)),
            jnp.transpose(from_odd[:, : col_count + FAR_RIGHT], (1, 0, 2)),
        ],
        axis=0,
    )

    samples_shape = (1, 1, samples)
    src_depth = levels[0].reshape(samples_shape)
    rcv_depth = levels[1].reshape(samples_shape)
    src_ends = jnp.stack([src_index == 0, src_index == src_count - 1]).astype(jnp.int32)
    rcv_ends = jnp.stack([rcv_index == 0, rcv_index == rcv_count - 1]).astype(jnp.int32)

    coeff = _call(
        functools.partial(_src_forward_kernel, width=SLOT, out_from=NEAR_LEFT),
        (NEAR_LEFT + row_count + NEAR_RIGHT, col_count, samples),
        [(row_count + 2 * SLOT + 2 * PAD, col_count, samples)],
        1,
        src_ends, src_depth, left_src, merged, right_src, mirror,
    )
    left_rcv, right_rcv = halos(coeff, "rcv", 1, FAR_LEFT, FAR_RIGHT)
    return _call(
        functools.partial(_rcv_kernel, width=SLOT, src_width=NEAR_SLOT, in_from=NEAR_LEFT),
        (row_count, col_count, samples),
        [
            (coeff.shape[0], col_count + 2 * SLOT + 2 * PAD, samples),
            (row_count + 2 * NEAR_SLOT + 2 * PAD, col_count, samples),
        ],
        2,
        rcv_ends, src_ends, rcv_depth, src_depth, thresholds.reshape(samples_shape),
        left_rcv, coeff, right_rcv,
    )

def solution(mesh):
    return jax.shard_map(
        body,
        mesh=mesh,
        in_specs=(P("src", "rcv", None), P("src", "rcv", None), P(), P(), P()),
        out_specs=P("src", "rcv", None),
        check_vma=False,
    )
```

```python
import functools

import jax
import jax.numpy as jnp
from jax import lax
from jax.sharding import PartitionSpec as P
from jax.experimental import pallas as pl
from jax.experimental.pallas import tpu as pltpu

LEVELS = 3
FAR_LEFT, FAR_RIGHT = 14, 15
NEAR_LEFT, NEAR_RIGHT = 4, 5
SLOT, NEAR_SLOT = 16, 8


PAD = 8


def _lift_level(work, stride, enabled, forward, width, length, ends, axis=0):
    rows = work.shape[axis] - 2 * PAD
    pairs = rows // (2 * stride)
    step = 2 * stride
    shape = list(work.shape)
    shape[axis] = pairs
    pair_ids = lax.broadcasted_iota(jnp.int32, tuple(shape), axis)
    first = (pair_ids == width // step) & (ends[0] != 0)
    last = (pair_ids == (width + length) // step - 1) & (ends[1] != 0)

    def at(start):
        window = pl.ds(start, pairs, stride=step)
        return (window,) if axis == 0 else (slice(None), window)

    evens = at(PAD)
    odds = at(PAD + stride)
    next_evens = at(PAD + step)
    prev_odds = at(PAD - stride)
    if forward:
        even_part = work[evens]
        odd_part = work[odds]
        next_even = jnp.where(last, even_part, work[next_evens])
        detail = odd_part - 0.5 * (even_part + next_even)
        work[odds] = jnp.where(enabled, detail, odd_part)
        prev_detail = jnp.where(first, detail, work[prev_odds])
        smooth = even_part + 0.25 * (prev_detail + detail)
        work[evens] = jnp.where(enabled, smooth, even_part)
    else:
        smooth = work[evens]
        detail = work[odds]
        prev_detail = jnp.where(first, detail, work[prev_odds])
        even_part = smooth - 0.25 * (prev_detail + detail)
        work[evens] = jnp.where(enabled, even_part, smooth)
        next_even = jnp.where(last, even_part, work[next_evens])
        odd_part = detail + 0.5 * (even_part + next_even)
        work[odds] = jnp.where(enabled, odd_part, detail)


def _fill(work, axis, parts, total):
    def span(lo, hi):
        return (slice(lo, hi),) if axis == 0 else (slice(None), slice(lo, hi))

    cursor = 0
    for offset, value in parts:
        if offset > cursor:
            shape = list(work.shape)
            shape[axis] = offset - cursor
            work[span(cursor, offset)] = jnp.zeros(shape, work.dtype)
        size = value.shape[axis]
        work[span(offset, offset + size)] = value
        cursor = offset + size
    if total > cursor:
        shape = list(work.shape)
        shape[axis] = total - cursor
        work[span(cursor, total)] = jnp.zeros(shape, work.dtype)


def _src_forward_kernel(
    ends_ref, depth_ref, left_ref, merged_ref, mirror_ref, right_ref, out_ref, tail_ref, head_ref, work,
    *, width, out_from,
):
    length = merged_ref.shape[0]
    ends = (ends_ref[0], ends_ref[1])
    depth = depth_ref[...]

    def half_sum(ref):
        return 0.5 * (ref[:, 0].astype(jnp.float32) + ref[:, 1].astype(jnp.float32))

    body = 0.5 * (merged_ref[...].astype(jnp.float32) + mirror_ref[...].astype(jnp.float32))
    parts = [
        (PAD + width - left_ref.shape[0], half_sum(left_ref)),
        (PAD + width, body),
        (PAD + width + length, half_sum(right_ref)),
    ]
    _fill(work, 0, parts, work.shape[0])
    for depth_index in range(LEVELS):
        _lift_level(work, 2**depth_index, depth > depth_index, True, width, length, ends)
    coeff = work[PAD + width - out_from : PAD + width - out_from + out_ref.shape[0]]
    out_ref[...] = coeff
    tail_ref[...] = coeff[:, coeff.shape[1] - tail_ref.shape[1] :]
    head_ref[...] = coeff[:, : head_ref.shape[1]]


def _rcv_kernel(
    rcv_ends_ref, src_ends_ref, rcv_depth_ref, src_depth_ref, thr_ref, left_ref, mid_ref, right_ref,
    out_ref, work, rows_work, *, width, src_width, in_from,
):
    length = mid_ref.shape[1]
    ends = (rcv_ends_ref[0], rcv_ends_ref[1])
    depth = rcv_depth_ref[...]
    parts = [
        (PAD + width - left_ref.shape[1], left_ref[...]),
        (PAD + width, mid_ref[...]),
        (PAD + width + length, right_ref[...]),
    ]
    _fill(work, 1, parts, work.shape[1])
    for depth_index in range(LEVELS):
        _lift_level(work, 2**depth_index, depth > depth_index, True, width, length, ends, axis=1)
    field = work[:, PAD : PAD + 2 * width + length]
    thr = thr_ref[...]
    work[:, PAD : PAD + 2 * width + length] = field - jnp.clip(field, -thr, thr)
    for depth_index in reversed(range(LEVELS)):
        _lift_level(work, 2**depth_index, depth > depth_index, False, width, length, ends, axis=1)

    row_count = out_ref.shape[0]
    ends = (src_ends_ref[0], src_ends_ref[1])
    depth = src_depth_ref[...]
    block = work[:, PAD + width : PAD + width + length]
    _fill(rows_work, 0, [(PAD + src_width - in_from, block)], rows_work.shape[0])
    for depth_index in reversed(range(LEVELS)):
        _lift_level(rows_work, 2**depth_index, depth > depth_index, False, src_width, row_count, ends)
    out_ref[...] = rows_work[PAD + src_width : PAD + src_width + row_count]


def _call(kernel, out_shape, scratch_shapes, smem_count, *operands):
    smem = pl.BlockSpec(memory_space=pltpu.SMEM)
    vmem = pl.BlockSpec(memory_space=pltpu.VMEM)
    several = isinstance(out_shape, list)
    shapes = out_shape if several else [out_shape]
    outs = [jax.ShapeDtypeStruct(shape, jnp.float32) for shape in shapes]
    return pl.pallas_call(
        kernel,
        out_shape=outs if several else outs[0],
        in_specs=[smem] * smem_count + [vmem] * (len(operands) - smem_count),
        out_specs=[vmem] * len(outs) if several else vmem,
        scratch_shapes=[pltpu.VMEM(shape, jnp.float32) for shape in scratch_shapes],
    )(*operands)


def halos(cells, axis_name, dim, left_width, right_width):
    length = cells.shape[dim]
    head = lax.slice_in_dim(cells, 0, right_width, axis=dim)
    tail = lax.slice_in_dim(cells, length - left_width, length, axis=dim)
    return swap(tail, head, axis_name)


def swap(tail, head, axis_name):
    count = lax.axis_size(axis_name)
    from_left = lax.ppermute(tail, axis_name, [(i, i + 1) for i in range(count - 1)])
    from_right = lax.ppermute(head, axis_name, [(i + 1, i) for i in range(count - 1)])
    return from_left, from_right


def body(observed, estimate, acquired, levels, thresholds):
    src_count = lax.axis_size("src")
    rcv_count = lax.axis_size("rcv")
    src_index = lax.axis_index("src")
    rcv_index = lax.axis_index("rcv")
    row_count, col_count, samples = observed.shape
    extent = row_count * src_count
    blocks = acquired.shape[0]
    block_size = extent // blocks
    block_ids = jnp.arange(blocks, dtype=jnp.int32)
    row_ids = src_index * row_count + jnp.arange(row_count, dtype=jnp.int32)
    col_ids = rcv_index * col_count + jnp.arange(col_count, dtype=jnp.int32)
    pick_rows = (row_ids[:, None] // block_size == block_ids[None, :]).astype(jnp.float32)
    pick_cols = (col_ids[:, None] // block_size == block_ids[None, :]).astype(jnp.float32)
    row_mask = jnp.dot(pick_rows, acquired.astype(jnp.float32), precision=lax.Precision.HIGHEST)
    local_mask = jnp.dot(row_mask, pick_cols.T, precision=lax.Precision.HIGHEST)
    est_float = estimate.astype(jnp.float32)
    merged = (
        est_float + local_mask[:, :, None] * (observed.astype(jnp.float32) - est_float)
    ).astype(jnp.bfloat16)

    ratio = rcv_count // src_count
    pieces = merged.reshape(ratio, col_count, col_count, samples)
    own_part = rcv_index % ratio
    received = []
    for shift in range(ratio):
        perm = []
        for a in range(src_count):
            for b in range(rcv_count):
                part = (b % ratio + shift) % ratio
                perm.append((a * rcv_count + b, (b // ratio) * rcv_count + a * ratio + part))
        send = lax.dynamic_index_in_dim(pieces, (own_part + shift) % ratio, axis=0, keepdims=False)
        received.append(lax.ppermute(send, ("src", "rcv"), perm))
    received = jnp.stack(received)
    slots = []
    for slot in range(ratio):
        got = lax.dynamic_index_in_dim(received, (own_part - slot) % ratio, axis=0, keepdims=False)
        slots.append(jnp.transpose(got, (1, 0, 2)))
    mirror = jnp.concatenate(slots, axis=0)
    samples_shape = (1, 1, samples)
    src_depth = levels[0].reshape(samples_shape)
    rcv_depth = levels[1].reshape(samples_shape)
    src_ends = jnp.stack([src_index == 0, src_index == src_count - 1]).astype(jnp.int32)
    rcv_ends = jnp.stack([rcv_index == 0, rcv_index == rcv_count - 1]).astype(jnp.int32)

    left_src, right_src = halos(jnp.stack([merged, mirror], axis=1), "src", 0, FAR_LEFT, FAR_RIGHT)
    coeff, tail, head = _call(
        functools.partial(_src_forward_kernel, width=SLOT, out_from=NEAR_LEFT),
        [
            (NEAR_LEFT + row_count + NEAR_RIGHT, col_count, samples),
            (NEAR_LEFT + row_count + NEAR_RIGHT, FAR_LEFT, samples),
            (NEAR_LEFT + row_count + NEAR_RIGHT, FAR_RIGHT, samples),
        ],
        [(row_count + 2 * SLOT + 2 * PAD, col_count, samples)],
        1,
        src_ends, src_depth, left_src, merged, mirror, right_src,
    )
    left_rcv, right_rcv = swap(tail, head, "rcv")
    return _call(
        functools.partial(_rcv_kernel, width=SLOT, src_width=NEAR_SLOT, in_from=NEAR_LEFT),
        (row_count, col_count, samples),
        [
            (coeff.shape[0], col_count + 2 * SLOT + 2 * PAD, samples),
            (row_count + 2 * NEAR_SLOT + 2 * PAD, col_count, samples),
        ],
        2,
        rcv_ends, src_ends, rcv_depth, src_depth, thresholds.reshape(samples_shape),
        left_rcv, coeff, right_rcv,
    )

def solution(mesh):
    return jax.shard_map(
        body,
        mesh=mesh,
        in_specs=(P("src", "rcv", None), P("src", "rcv", None), P(), P(), P()),
        out_specs=P("src", "rcv", None),
        check_vma=False,
    )
```

```python
import functools

import jax
import jax.numpy as jnp
from jax import lax
from jax.sharding import PartitionSpec as P
from jax.experimental import pallas as pl
from jax.experimental.pallas import tpu as pltpu

LEVELS = 3
FAR_LEFT, FAR_RIGHT = 14, 15
NEAR_LEFT, NEAR_RIGHT = 4, 5
SLOT, NEAR_SLOT = 16, 8


PAD = 8


def _lift_level(work, stride, enabled, forward, width, length, ends, axis=0):
    rows = work.shape[axis] - 2 * PAD
    pairs = rows // (2 * stride)
    step = 2 * stride
    shape = list(work.shape)
    shape[axis] = pairs
    pair_ids = lax.broadcasted_iota(jnp.int32, tuple(shape), axis)
    first = (pair_ids == width // step) & ends[0]
    last = (pair_ids == (width + length) // step - 1) & ends[1]

    def at(start):
        window = pl.ds(start, pairs, stride=step)
        return (window,) if axis == 0 else (slice(None), window)

    evens = at(PAD)
    odds = at(PAD + stride)
    next_evens = at(PAD + step)
    prev_odds = at(PAD - stride)
    if forward:
        even_part = work[evens]
        odd_part = work[odds]
        next_even = jnp.where(last, even_part, work[next_evens])
        detail = odd_part - 0.5 * (even_part + next_even)
        work[odds] = jnp.where(enabled, detail, odd_part)
        prev_detail = jnp.where(first, detail, work[prev_odds])
        smooth = even_part + 0.25 * (prev_detail + detail)
        work[evens] = jnp.where(enabled, smooth, even_part)
    else:
        smooth = work[evens]
        detail = work[odds]
        prev_detail = jnp.where(first, detail, work[prev_odds])
        even_part = smooth - 0.25 * (prev_detail + detail)
        work[evens] = jnp.where(enabled, even_part, smooth)
        next_even = jnp.where(last, even_part, work[next_evens])
        odd_part = detail + 0.5 * (even_part + next_even)
        work[odds] = jnp.where(enabled, odd_part, detail)


def _ends(axis_name):
    index = lax.axis_index(axis_name)
    return (index == 0, index == lax.axis_size(axis_name) - 1)


def _fill(work, axis, parts, total):
    def span(lo, hi):
        return (slice(lo, hi),) if axis == 0 else (slice(None), slice(lo, hi))

    cursor = 0
    for offset, value in parts:
        if offset > cursor:
            shape = list(work.shape)
            shape[axis] = offset - cursor
            work[span(cursor, offset)] = jnp.zeros(shape, work.dtype)
        size = value.shape[axis]
        work[span(offset, offset + size)] = value
        cursor = offset + size
    if total > cursor:
        shape = list(work.shape)
        shape[axis] = total - cursor
        work[span(cursor, total)] = jnp.zeros(shape, work.dtype)


def _src_forward_kernel(
    depth_ref, left_ref, merged_ref, mirror_ref, right_ref, out_ref, tail_ref, head_ref, work,
    *, width, out_from,
):
    length = merged_ref.shape[0]
    ends = _ends("src")
    depth = depth_ref[...]

    def half_sum(ref):
        return 0.5 * (ref[:, 0].astype(jnp.float32) + ref[:, 1].astype(jnp.float32))

    body = 0.5 * (merged_ref[...].astype(jnp.float32) + mirror_ref[...].astype(jnp.float32))
    parts = [
        (PAD + width - left_ref.shape[0], half_sum(left_ref)),
        (PAD + width, body),
        (PAD + width + length, half_sum(right_ref)),
    ]
    _fill(work, 0, parts, work.shape[0])
    for depth_index in range(LEVELS):
        _lift_level(work, 2**depth_index, depth > depth_index, True, width, length, ends)
    coeff = work[PAD + width - out_from : PAD + width - out_from + out_ref.shape[0]]
    out_ref[...] = coeff
    tail_ref[...] = coeff[:, coeff.shape[1] - tail_ref.shape[1] :]
    head_ref[...] = coeff[:, : head_ref.shape[1]]


def _rcv_kernel(
    rcv_depth_ref, src_depth_ref, thr_ref, left_ref, mid_ref, right_ref,
    out_ref, work, rows_work, *, width, src_width, in_from,
):
    length = mid_ref.shape[1]
    ends = _ends("rcv")
    depth = rcv_depth_ref[...]
    parts = [
        (PAD + width - left_ref.shape[1], left_ref[...]),
        (PAD + width, mid_ref[...]),
        (PAD + width + length, right_ref[...]),
    ]
    _fill(work, 1, parts, work.shape[1])
    for depth_index in range(LEVELS):
        _lift_level(work, 2**depth_index, depth > depth_index, True, width, length, ends, axis=1)
    field = work[:, PAD : PAD + 2 * width + length]
    thr = thr_ref[...]
    work[:, PAD : PAD + 2 * width + length] = field - jnp.clip(field, -thr, thr)
    for depth_index in reversed(range(LEVELS)):
        _lift_level(work, 2**depth_index, depth > depth_index, False, width, length, ends, axis=1)

    row_count = out_ref.shape[0]
    ends = _ends("src")
    depth = src_depth_ref[...]
    block = work[:, PAD + width : PAD + width + length]
    _fill(rows_work, 0, [(PAD + src_width - in_from, block)], rows_work.shape[0])
    for depth_index in reversed(range(LEVELS)):
        _lift_level(rows_work, 2**depth_index, depth > depth_index, False, src_width, row_count, ends)
    out_ref[...] = rows_work[PAD + src_width : PAD + src_width + row_count]


def _call(kernel, out_shape, scratch_shapes, smem_count, *operands):
    smem = pl.BlockSpec(memory_space=pltpu.SMEM)
    vmem = pl.BlockSpec(memory_space=pltpu.VMEM)
    several = isinstance(out_shape, list)
    shapes = out_shape if several else [out_shape]
    outs = [jax.ShapeDtypeStruct(shape, jnp.float32) for shape in shapes]
    return pl.pallas_call(
        kernel,
        out_shape=outs if several else outs[0],
        in_specs=[smem] * smem_count + [vmem] * (len(operands) - smem_count),
        out_specs=[vmem] * len(outs) if several else vmem,
        scratch_shapes=[pltpu.VMEM(shape, jnp.float32) for shape in scratch_shapes],
    )(*operands)


def halos(cells, axis_name, dim, left_width, right_width):
    length = cells.shape[dim]
    head = lax.slice_in_dim(cells, 0, right_width, axis=dim)
    tail = lax.slice_in_dim(cells, length - left_width, length, axis=dim)
    return swap(tail, head, axis_name)


def swap(tail, head, axis_name):
    count = lax.axis_size(axis_name)
    from_left = lax.ppermute(tail, axis_name, [(i, i + 1) for i in range(count - 1)])
    from_right = lax.ppermute(head, axis_name, [(i + 1, i) for i in range(count - 1)])
    return from_left, from_right


def body(observed, estimate, acquired, levels, thresholds):
    src_count = lax.axis_size("src")
    rcv_count = lax.axis_size("rcv")
    src_index = lax.axis_index("src")
    rcv_index = lax.axis_index("rcv")
    row_count, col_count, samples = observed.shape
    extent = row_count * src_count
    blocks = acquired.shape[0]
    block_size = extent // blocks
    block_ids = jnp.arange(blocks, dtype=jnp.int32)
    row_ids = src_index * row_count + jnp.arange(row_count, dtype=jnp.int32)
    col_ids = rcv_index * col_count + jnp.arange(col_count, dtype=jnp.int32)
    pick_rows = (row_ids[:, None] // block_size == block_ids[None, :]).astype(jnp.float32)
    pick_cols = (col_ids[:, None] // block_size == block_ids[None, :]).astype(jnp.float32)
    row_mask = jnp.dot(pick_rows, acquired.astype(jnp.float32), precision=lax.Precision.HIGHEST)
    local_mask = jnp.dot(row_mask, pick_cols.T, precision=lax.Precision.HIGHEST)
    est_float = estimate.astype(jnp.float32)
    merged = (
        est_float + local_mask[:, :, None] * (observed.astype(jnp.float32) - est_float)
    ).astype(jnp.bfloat16)

    ratio = rcv_count // src_count
    pieces = merged.reshape(ratio, col_count, col_count, samples)
    own_part = rcv_index % ratio
    received = []
    for shift in range(ratio):
        perm = []
        for a in range(src_count):
            for b in range(rcv_count):
                part = (b % ratio + shift) % ratio
                perm.append((a * rcv_count + b, (b // ratio) * rcv_count + a * ratio + part))
        send = lax.dynamic_index_in_dim(pieces, (own_part + shift) % ratio, axis=0, keepdims=False)
        received.append(lax.ppermute(send, ("src", "rcv"), perm))
    received = jnp.stack(received)
    slots = []
    for slot in range(ratio):
        got = lax.dynamic_index_in_dim(received, (own_part - slot) % ratio, axis=0, keepdims=False)
        slots.append(jnp.transpose(got, (1, 0, 2)))
    mirror = jnp.concatenate(slots, axis=0)
    samples_shape = (1, 1, samples)
    src_depth = levels[0].reshape(samples_shape)
    rcv_depth = levels[1].reshape(samples_shape)

    left_src, right_src = halos(jnp.stack([merged, mirror], axis=1), "src", 0, FAR_LEFT, FAR_RIGHT)
    coeff, tail, head = _call(
        functools.partial(_src_forward_kernel, width=SLOT, out_from=NEAR_LEFT),
        [
            (NEAR_LEFT + row_count + NEAR_RIGHT, col_count, samples),
            (NEAR_LEFT + row_count + NEAR_RIGHT, FAR_LEFT, samples),
            (NEAR_LEFT + row_count + NEAR_RIGHT, FAR_RIGHT, samples),
        ],
        [(row_count + 2 * SLOT + 2 * PAD, col_count, samples)],
        0,
        src_depth, left_src, merged, mirror, right_src,
    )
    left_rcv, right_rcv = swap(tail, head, "rcv")
    return _call(
        functools.partial(_rcv_kernel, width=SLOT, src_width=NEAR_SLOT, in_from=NEAR_LEFT),
        (row_count, col_count, samples),
        [
            (coeff.shape[0], col_count + 2 * SLOT + 2 * PAD, samples),
            (row_count + 2 * NEAR_SLOT + 2 * PAD, col_count, samples),
        ],
        0,
        rcv_depth, src_depth, thresholds.reshape(samples_shape),
        left_rcv, coeff, right_rcv,
    )

def solution(mesh):
    return jax.shard_map(
        body,
        mesh=mesh,
        in_specs=(P("src", "rcv", None), P("src", "rcv", None), P(), P(), P()),
        out_specs=P("src", "rcv", None),
        check_vma=False,
    )
```
